256 devices in a mesh: lon: 64 (over y, z, x_hi), lat: 4 (over x_lo, core).
Axes of the slice: x: 4 (x_hi: 2, x_lo: 2; x = x_hi * 2 + x_lo), y: 4, z: 8, core: 2. Of those that a mesh axis runs over, the one named last changes fastest.
Arguments:
- initial_state: float32 [4, 32, 1024, 512], P(None, None, 'lon', 'lat'), may hold values from -6 to 6
- coefficients: float32 [4, 32, 1024, 512], P(None, None, 'lon', 'lat'), may hold values from 0.02 to 0.24
- coupling: float32 [32, 4, 4], replicated, may hold values from -3 to 3
- obs_band: int32 [4, 32768, 1], P('lat', 'lon'), may hold values from 0 to 63; in each aligned block of 512 rows (0 to 511, 512 to 1023, ..., all dimensions but the last counted through in order) at most 32 rows name the same one
- obs_cell: int32 [4, 32768], P('lat', 'lon'), may hold values from 0 to 262143
- obs_value: float32 [4, 32768], P('lat', 'lon'), may hold values from -6 to 6
- obs_weight: float32 [4, 32768], P('lat', 'lon'), may hold values from 0.5 to 4
- obs_count: int32 [4, 64], P('lat', 'lon'), may hold values from 256 to 512
Outputs:
- final_state: float32 [4, 32, 1024, 512], P(None, None, 'lon', 'lat')
- gradient: float32 [4, 32, 1024, 512], P(None, None, 'lon', 'lat')
The draws below stay inside these ranges and needn't reach their ends.
Inputs may be any that keep to these rules, and one draw needn't show every extreme that they name: `obs_band`: in the 512 rows of one device no band is named more than 32 times, a bound that some block reaches.
All inputs are finite; a program needn't handle non-finite values.
Results may differ from the reference program's by a relative error of at most 0.0003.
Values sent between devices are 32-bit elements; how exact they have to be, the bound alone decides.
No kernel may reach another device: no remote copies, remote signals or barrier semaphores. Data moves between devices by JAX's collectives and lax.ppermute only.
A program may use at most 128 MiB of HBM per device.

```python
import math
import jax
import jax.numpy as jnp
import numpy as np
from jax import lax

FIELDS = 4
LEV = 32
STEPS = 2
CLAT = 128
CLON = 16
NOBS_DEV = 512
NLAT = 512
NLON = 1024
CAP = 32
CELLS = 262144
N_LON = 64
N_LAT = 4


def with_ends(drawn, own_key, smallest, high):
    place = [jax.random.randint(jax.random.fold_in(own_key, axis), (), 0, length) for axis, length in enumerate(drawn.shape)]
    main_axis = drawn.shape.index(max(drawn.shape))
    beside = place[:main_axis] + [(place[main_axis] + 1) % drawn.shape[main_axis]] + place[main_axis + 1:]
    return drawn.at[tuple(place)].set(smallest).at[tuple(beside)].set(high)


def level_of(own_key, shape, cuts, smallest, high):
    loudness, own = 1.0, jax.random.fold_in(own_key, 6)
    for axis_at, shards_of in cuts:
        steps = jnp.exp(jax.random.uniform(jax.random.fold_in(own, axis_at), (shards_of,), jnp.float32, smallest / len(cuts), high / len(cuts)))
        loudness = loudness * jnp.repeat(steps, shape[axis_at] // shards_of).reshape([-1 if axis == axis_at else 1 for axis in range(len(shape))])
    return loudness


def deal_out(own_key, own, number, rows, amount, top, most, skew):
    sequence = jax.random.permutation(own_key, amount)
    packed, ordinary = shares(amount, rows * top, most, skew, True), shares(amount, rows * top, most, skew, False)
    places = jnp.arange(amount)

    def named(lengths, rotation):
        used = int((lengths > 0).sum())
        fixed = max(1, used // 4)
        passed = fixed + (places - fixed + rotation * (used - fixed)) % max(1, amount - fixed)
        return jnp.zeros((amount,), jnp.int32).at[sequence[jnp.where(places < fixed, places, passed)]].set(jnp.asarray(lengths, jnp.int32))

    lengths = jnp.where(number % 4 == 0, named(packed, number // 4), named(ordinary, number - number // 4 - 1))
    mixed = jax.random.permutation(jax.random.fold_in(own, 3), amount)
    giver, taker = mixed[0:amount // 2 * 2:2], mixed[1:amount // 2 * 2:2]
    room = jnp.minimum(lengths[giver] - 1, most - lengths[taker]) // 2
    room = jnp.where((giver == sequence[0]) | (taker == sequence[0]) | (lengths[taker] == 0), 0, jnp.maximum(room, 0))
    passed = jax.random.randint(jax.random.fold_in(own, 4), (amount // 2,), 0, 1 << 20) % (room + 1)
    lengths = lengths.at[giver].add(-passed).at[taker].add(passed)
    members = jnp.searchsorted(jnp.cumsum(lengths), jnp.arange(rows * top), side="right").astype(jnp.int32)
    listing = members.reshape(top, rows).T
    listing = listing[jax.random.permutation(jax.random.fold_in(own, 1), rows)]
    rotation = jax.random.randint(jax.random.fold_in(own, 2), (rows, 1), 0, top)
    return jnp.take_along_axis(listing, (jnp.arange(top)[None, :] + rotation) % top, axis=1)


def shares(count, total, most, slope, full):
    loads = [(1 << 20) // math.isqrt(grade ** slope) + 1 for grade in range(1, count + 1)]
    largest = most if full else min(most, max(-(-total // count), total * loads[0] // sum(loads)))
    least = 1 if total - largest >= count - 1 else 0
    given, spare = [largest] + [least] * (count - 1), total - largest - least * (count - 1)
    while spare > 0:
        movable = [i for i in range(1, count) if given[i] < largest] or [i for i in range(1, count) if given[i] < most]
        mass, left = sum([loads[i] for i in movable]), spare
        for i in movable:
            addition = min(most - given[i], max(1, left * loads[i] // mass), spare)
            given[i] = given[i] + addition
            spare = spare - addition
    return np.array(given)


def gaussian(stream_key, dims, deviation, bound, split=(), held_as=jnp.bfloat16):
    drawn = deviation * jax.random.normal(stream_key, dims, jnp.float32)
    if split:
        drawn = drawn * level_of(stream_key, dims, split, -0.22, 0.18)
    return jnp.clip(drawn, -bound, bound).astype(held_as)


def setup_inputs(seed: int = 0) -> dict:
    streams_of = jax.random.split(jax.random.key(seed), 9)
    initial_state = gaussian(streams_of[0], (FIELDS, LEV, NLON, NLAT), 1.0, 6.0, ((2, 64), (3, 4)), jnp.float32)
    coefficients = jnp.clip(0.02 + 0.22 * jax.random.uniform(streams_of[1], (4, LEV, NLON, NLAT), jnp.float32) ** level_of(streams_of[1], (4, LEV, NLON, NLAT), ((2, 64), (3, 4)), -0.2, 0.2), 0.02, 0.24)
    coupling = gaussian(streams_of[2], (LEV, FIELDS, FIELDS), FIELDS ** -0.5, 3.0, (), jnp.float32)
    obs_band_keys = jax.random.split(jax.random.fold_in(streams_of[3], 1), N_LAT * (N_LON * NOBS_DEV) // NOBS_DEV)
    obs_band_turns = jax.random.permutation(jax.random.fold_in(streams_of[3], 3), N_LAT * (N_LON * NOBS_DEV) // NOBS_DEV)
    obs_band = jax.vmap(lambda own, number: deal_out(jax.random.fold_in(streams_of[3], 2), own, number, NOBS_DEV, N_LON, 1, CAP, 2))(obs_band_keys, obs_band_turns).reshape((N_LAT, N_LON * NOBS_DEV, 1))
    obs_cell = with_ends(jax.random.randint(streams_of[4], (N_LAT, N_LON * NOBS_DEV), 0, CELLS), jax.random.fold_in(streams_of[4], 1), 0, CELLS - 1).astype(jnp.int32)
    obs_value = gaussian(streams_of[5], (N_LAT, N_LON * NOBS_DEV), 1.0, 6.0, ((0, 4), (1, 64)), jnp.float32)
    obs_weight = jnp.clip(jnp.exp(math.log(4.0) - 2.0794415 * jax.random.uniform(streams_of[6], (N_LAT, N_LON * NOBS_DEV), jnp.float32) ** level_of(streams_of[6], (N_LAT, N_LON * NOBS_DEV), ((0, 4), (1, 64)), -0.2, 0.2)), 0.5, 4.0)
    obs_count = with_ends(jax.random.randint(streams_of[7], (N_LAT, N_LON), NOBS_DEV // 2, NOBS_DEV + 1), jax.random.fold_in(streams_of[7], 1), NOBS_DEV // 2, NOBS_DEV).astype(jnp.int32)
    return {"initial_state": initial_state, "coefficients": coefficients, "coupling": coupling, "obs_band": obs_band, "obs_cell": obs_cell, "obs_value": obs_value, "obs_weight": obs_weight, "obs_count": obs_count}


def neighbour_set(x):
    half = x.shape[2] // 2
    flip = jnp.array([-1.0, -1.0, 1.0, 1.0], dtype=x.dtype).reshape(4, 1, 1, 1)
    top = flip * jnp.roll(x[:, :, :, 0:1], half, axis=2)
    bottom = flip * jnp.roll(x[:, :, :, -1:], half, axis=2)
    north = jnp.concatenate([top, x[:, :, :, :-1]], axis=3)
    south = jnp.concatenate([x[:, :, :, 1:], bottom], axis=3)
    west = jnp.roll(x, 1, axis=2)
    east = jnp.roll(x, -1, axis=2)
    return (north, south, west, east)

def model_step(x, coefficients, coupling):
    north, south, west, east = neighbour_set(x)
    total = coefficients[0] + coefficients[1] + coefficients[2] + coefficients[3]
    mixed = jnp.einsum('lgf,flij->glij', coupling, x, precision=lax.Precision.HIGHEST)
    y = x + coefficients[0] * north + coefficients[1] * south + coefficients[2] * west + coefficients[3] * east - total * x + 0.25 * mixed
    return y - 0.5 * jnp.tanh(y)

def reference(initial_state, coefficients, coupling, obs_band, obs_cell, obs_value, obs_weight, obs_count):
    states = [initial_state]
    x = initial_state
    for step in range(STEPS):
        x = model_step(x, coefficients, coupling)
        states.append(x)
    final_state = x
    n_lat = obs_cell.shape[0]
    rows = obs_cell.shape[1]
    per_dev = rows // (final_state.shape[2] // CLON)
    row_ids = jnp.arange(rows, dtype=jnp.int32)
    source = row_ids // per_dev
    local_row = row_ids % per_dev
    block_ids = jnp.arange(n_lat, dtype=jnp.int32)[:, None]
    counts = jnp.take_along_axis(obs_count, jnp.broadcast_to(source[None, :], (n_lat, rows)), axis=1)
    valid = (local_row[None, :] < counts).astype(jnp.float32)
    cell = obs_cell
    field = cell // (LEV * CLON * CLAT)
    level = cell // (CLON * CLAT) % LEV
    glon = obs_band[:, :, 0] * CLON + cell // CLAT % CLON
    glat = block_ids * CLAT + cell % CLAT
    picked = final_state[field, level, glon, glat]
    forcing = valid * obs_weight * (picked - obs_value)
    lam = jnp.zeros_like(final_state).at[field, level, glon, glat].add(forcing)
    for step in range(STEPS - 1, -1, -1):
        out, pullback = jax.vjp(lambda v: model_step(v, coefficients, coupling), states[step])
        lam = pullback(lam)[0]
    return (final_state, lam)
```

```python
import jax
import jax.numpy as jnp
from jax import lax
from jax.sharding import PartitionSpec as P

STEPS = 2
CAP = 32


def ring_pairs(n_lon, n_lat):
    half = n_lon // 2
    pairs = []
    for i in range(half):
        ring = [(i, j) for j in range(n_lat)] + [(i + half, j) for j in range(n_lat - 1, -1, -1)]
        for k in range(len(ring)):
            a, b = ring[k], ring[(k + 1) % len(ring)]
            pairs.append((a[0] * n_lat + a[1], b[0] * n_lat + b[1]))
    return pairs


def halos(x, flip):
    n_lon = lax.axis_size("lon")
    n_lat = lax.axis_size("lat")
    lon_i = lax.axis_index("lon")
    lat_j = lax.axis_index("lat")
    up = [(i, (i + 1) % n_lon) for i in range(n_lon)]
    down = [(b, a) for a, b in up]
    from_west = lax.ppermute(x[:, :, -1, :], "lon", up)
    from_east = lax.ppermute(x[:, :, 0, :], "lon", down)
    low = lon_i < n_lon // 2
    first_row = x[:, :, :, 0]
    last_row = x[:, :, :, -1]
    cw_pairs = ring_pairs(n_lon, n_lat)
    ccw_pairs = [(b, a) for a, b in cw_pairs]
    cw = lax.ppermute(jnp.where(low, last_row, first_row), ("lon", "lat"), cw_pairs)
    ccw = lax.ppermute(jnp.where(low, first_row, last_row), ("lon", "lat"), ccw_pairs)
    north_row = jnp.where(low, cw, ccw)
    south_row = jnp.where(low, ccw, cw)
    north_row = jnp.where(lat_j == 0, flip * north_row, north_row)
    south_row = jnp.where(lat_j == n_lat - 1, flip * south_row, south_row)
    return north_row, south_row, from_west, from_east


def shifted(x, halo):
    north_row, south_row, from_west, from_east = halo
    north = jnp.concatenate([north_row[..., None], x[..., :-1]], axis=3)
    south = jnp.concatenate([x[..., 1:], south_row[..., None]], axis=3)
    west = jnp.concatenate([from_west[:, :, None, :], x[:, :, :-1, :]], axis=2)
    east = jnp.concatenate([x[:, :, 1:, :], from_east[:, :, None, :]], axis=2)
    return north, south, west, east


def mix(coupling, v, transpose):
    out = []
    for g in range(v.shape[0]):
        acc = None
        for f in range(v.shape[0]):
            c = coupling[:, f, g] if transpose else coupling[:, g, f]
            term = c[:, None, None] * v[f]
            acc = term if acc is None else acc + term
        out.append(acc)
    return jnp.stack(out)


def on_device(
    initial_state, coefficients, coupling, obs_band, obs_cell, obs_value, obs_weight, obs_count
):
    wind_flip = jnp.array([-1.0, -1.0, 1.0, 1.0], dtype=jnp.float32).reshape(4, 1, 1)
    plain_flip = jnp.ones((4, 1, 1), jnp.float32)
    total = coefficients[0] + coefficients[1] + coefficients[2] + coefficients[3]
    stored = []
    x = initial_state
    for step in range(STEPS):
        n, s, w, e = shifted(x, halos(x, wind_flip))
        y = (
            x
            + coefficients[0] * n
            + coefficients[1] * s
            + coefficients[2] * w
            + coefficients[3] * e
            - total * x
            + 0.25 * mix(coupling, x, False)
        )
        stored.append(y)
        x = y - 0.5 * jnp.tanh(y)

    n_lon = lax.axis_size("lon")
    rows = obs_cell.shape[1]
    band = obs_band[0, :, 0]
    valid = jnp.arange(rows, dtype=jnp.int32) < obs_count[0, 0]
    weight = jnp.where(valid, obs_weight[0], 0.0)
    ids = jnp.arange(rows, dtype=jnp.int32)
    same = (band[:, None] == band[None, :]) & (ids[None, :] < ids[:, None])
    rank = jnp.sum(same.astype(jnp.int32), axis=1)
    slot = band * CAP + rank
    payload = jnp.stack([obs_value[0], weight, obs_cell[0].astype(jnp.float32)], axis=1)
    slots = jnp.arange(n_lon * CAP, dtype=jnp.int32)
    hit = slot[None, :] == slots[:, None]
    send = jnp.sum(jnp.where(hit[:, :, None], payload[None, :, :], 0.0), axis=1)
    arrived = lax.all_to_all(send, "lon", 0, 0, tiled=True)
    values = arrived[:, 0]
    weights = arrived[:, 1]
    cells = arrived[:, 2].astype(jnp.int32)
    lanes = x.shape[3]
    row_of = cells // lanes
    lane_of = cells % lanes
    table = x.reshape(-1, lanes)
    lane_hit = lane_of[:, None] == jnp.arange(lanes, dtype=jnp.int32)[None, :]
    picked = jnp.sum(jnp.where(lane_hit, table[row_of], 0.0), axis=1)
    forcing = weights * (picked - values)
    spread = jnp.where(lane_hit, forcing[:, None], 0.0)
    lam = jnp.zeros_like(table).at[row_of].add(spread).reshape(x.shape)

    near_n, near_s, near_w, near_e = shifted(coefficients, halos(coefficients, plain_flip))
    row_ids = jnp.arange(coefficients.shape[3], dtype=jnp.int32)[None, :]
    polar_top = (lax.axis_index("lat") == 0) & (row_ids == 0)
    polar_bottom = (lax.axis_index("lat") == lax.axis_size("lat") - 1) & (
        row_ids == coefficients.shape[3] - 1
    )
    from_north = jnp.where(polar_top, near_n[0], near_n[1])
    from_south = jnp.where(polar_bottom, near_s[1], near_s[0])
    from_west = near_w[3]
    from_east = near_e[2]
    for step in range(STEPS - 1, -1, -1):
        squashed = jnp.tanh(stored[step])
        lam_y = lam * (1.0 - 0.5 * (1.0 - squashed * squashed))
        north, south, west, east = shifted(lam_y, halos(lam_y, wind_flip))
        lam = (
            lam_y
            - total * lam_y
            + 0.25 * mix(coupling, lam_y, True)
            + from_north * north
            + from_south * south
            + from_west * west
            + from_east * east
        )
    return (x, lam)


def solution(mesh):
    in_specs = (
        P(None, None, "lon", "lat"),
        P(None, None, "lon", "lat"),
        P(),
        P("lat", "lon", None),
        P("lat", "lon"),
        P("lat", "lon"),
        P("lat", "lon"),
        P("lat", "lon"),
    )
    out_specs = (P(None, None, "lon", "lat"), P(None, None, "lon", "lat"))
    return jax.shard_map(
        on_device, mesh=mesh, in_specs=in_specs, out_specs=out_specs, check_vma=False
    )
```

```python
import jax
import jax.numpy as jnp
from jax import lax
from jax.sharding import PartitionSpec as P

STEPS = 2
CAP = 32


def ring_pairs(n_lon, n_lat):
    half = n_lon // 2
    pairs = []
    for i in range(half):
        ring = [(i, j) for j in range(n_lat)] + [(i + half, j) for j in range(n_lat - 1, -1, -1)]
        for k in range(len(ring)):
            a, b = ring[k], ring[(k + 1) % len(ring)]
            pairs.append((a[0] * n_lat + a[1], b[0] * n_lat + b[1]))
    return pairs


def halos(x, flip):
    n_lon = lax.axis_size("lon")
    n_lat = lax.axis_size("lat")
    lon_i = lax.axis_index("lon")
    lat_j = lax.axis_index("lat")
    up = [(i, (i + 1) % n_lon) for i in range(n_lon)]
    down = [(b, a) for a, b in up]
    from_west = lax.ppermute(x[:, :, -1, :], "lon", up)
    from_east = lax.ppermute(x[:, :, 0, :], "lon", down)
    low = lon_i < n_lon // 2
    first_row = x[:, :, :, 0]
    last_row = x[:, :, :, -1]
    cw_pairs = ring_pairs(n_lon, n_lat)
    ccw_pairs = [(b, a) for a, b in cw_pairs]
    cw = lax.ppermute(jnp.where(low, last_row, first_row), ("lon", "lat"), cw_pairs)
    ccw = lax.ppermute(jnp.where(low, first_row, last_row), ("lon", "lat"), ccw_pairs)
    north_row = jnp.where(low, cw, ccw)
    south_row = jnp.where(low, ccw, cw)
    north_row = jnp.where(lat_j == 0, flip * north_row, north_row)
    south_row = jnp.where(lat_j == n_lat - 1, flip * south_row, south_row)
    return north_row, south_row, from_west, from_east


def shifted(x, halo):
    north_row, south_row, from_west, from_east = halo
    north = jnp.concatenate([north_row[..., None], x[..., :-1]], axis=3)
    south = jnp.concatenate([x[..., 1:], south_row[..., None]], axis=3)
    west = jnp.concatenate([from_west[:, :, None, :], x[:, :, :-1, :]], axis=2)
    east = jnp.concatenate([x[:, :, 1:, :], from_east[:, :, None, :]], axis=2)
    return north, south, west, east


def mix(coupling, v, transpose):
    acc = None
    for f in range(v.shape[0]):
        c = coupling[:, f, :] if transpose else coupling[:, :, f]
        term = jnp.transpose(c)[:, :, None, None] * v[f][None]
        acc = term if acc is None else acc + term
    return acc


def on_device(
    initial_state, coefficients, coupling, obs_band, obs_cell, obs_value, obs_weight, obs_count
):
    wind_flip = jnp.array([-1.0, -1.0, 1.0, 1.0], dtype=jnp.float32).reshape(4, 1, 1)
    plain_flip = jnp.ones((4, 1, 1), jnp.float32)
    total = coefficients[0] + coefficients[1] + coefficients[2] + coefficients[3]
    stored = []
    x = initial_state
    both_flip = jnp.concatenate([wind_flip, plain_flip])
    joint = halos(jnp.concatenate([x, coefficients]), both_flip)
    first_halo = tuple(h[:4] for h in joint)
    coef_halo = tuple(h[4:] for h in joint)
    for step in range(STEPS):
        n, s, w, e = shifted(x, first_halo if step == 0 else halos(x, wind_flip))
        y = (
            x
            + coefficients[0] * n
            + coefficients[1] * s
            + coefficients[2] * w
            + coefficients[3] * e
            - total * x
            + 0.25 * mix(coupling, x, False)
        )
        stored.append(y)
        x = y - 0.5 * jnp.tanh(y)

    n_lon = lax.axis_size("lon")
    rows = obs_cell.shape[1]
    band = obs_band[0, :, 0]
    valid = jnp.arange(rows, dtype=jnp.int32) < obs_count[0, 0]
    weight = jnp.where(valid, obs_weight[0], 0.0)
    ids = jnp.arange(rows, dtype=jnp.int32)
    same = (band[:, None] == band[None, :]) & (ids[None, :] < ids[:, None])
    rank = jnp.sum(same.astype(jnp.int32), axis=1)
    slot = band * CAP + rank
    payload = jnp.stack([obs_value[0], weight, obs_cell[0].astype(jnp.float32)], axis=1)
    slots = jnp.arange(n_lon * CAP, dtype=jnp.int32)
    hit = slot[None, :] == slots[:, None]
    send = jnp.sum(jnp.where(hit[:, :, None], payload[None, :, :], 0.0), axis=1)
    arrived = lax.all_to_all(send, "lon", 0, 0, tiled=True)
    values = arrived[:, 0]
    weights = arrived[:, 1]
    cells = arrived[:, 2].astype(jnp.int32)
    lanes = x.shape[3]
    row_of = cells // lanes
    lane_of = cells % lanes
    table = x.reshape(-1, lanes)
    lane_hit = lane_of[:, None] == jnp.arange(lanes, dtype=jnp.int32)[None, :]
    picked = jnp.sum(jnp.where(lane_hit, table[row_of], 0.0), axis=1)
    forcing = weights * (picked - values)
    spread = jnp.where(lane_hit, forcing[:, None], 0.0)
    lam = jnp.zeros_like(table).at[row_of].add(spread).reshape(x.shape)

    near_n, near_s, near_w, near_e = shifted(coefficients, coef_halo)
    row_ids = jnp.arange(coefficients.shape[3], dtype=jnp.int32)[None, :]
    polar_top = (lax.axis_index("lat") == 0) & (row_ids == 0)
    polar_bottom = (lax.axis_index("lat") == lax.axis_size("lat") - 1) & (
        row_ids == coefficients.shape[3] - 1
    )
    from_north = jnp.where(polar_top, near_n[0], near_n[1])
    from_south = jnp.where(polar_bottom, near_s[1], near_s[0])
    from_west = near_w[3]
    from_east = near_e[2]
    for step in range(STEPS - 1, -1, -1):
        squashed = jnp.tanh(stored[step])
        lam_y = lam * (1.0 - 0.5 * (1.0 - squashed * squashed))
        north, south, west, east = shifted(lam_y, halos(lam_y, wind_flip))
        lam = (
            lam_y
            - total * lam_y
            + 0.25 * mix(coupling, lam_y, True)
            + from_north * north
            + from_south * south
            + from_west * west
            + from_east * east
        )
    return (x, lam)


def solution(mesh):
    in_specs = (
        P(None, None, "lon", "lat"),
        P(None, None, "lon", "lat"),
        P(),
        P("lat", "lon", None),
        P("lat", "lon"),
        P("lat", "lon"),
        P("lat", "lon"),
        P("lat", "lon"),
    )
    out_specs = (P(None, None, "lon", "lat"), P(None, None, "lon", "lat"))
    return jax.shard_map(
        on_device, mesh=mesh, in_specs=in_specs, out_specs=out_specs, check_vma=False
    )
```

```python
import jax
import jax.numpy as jnp
from jax import lax
from jax.sharding import PartitionSpec as P
from jax.experimental import pallas as pl
from jax.experimental.pallas import tpu as pltpu

STEPS = 2
CAP = 32


def ring_pairs(n_lon, n_lat):
    half = n_lon // 2
    pairs = []
    for i in range(half):
        ring = [(i, j) for j in range(n_lat)] + [(i + half, j) for j in range(n_lat - 1, -1, -1)]
        for k in range(len(ring)):
            a, b = ring[k], ring[(k + 1) % len(ring)]
            pairs.append((a[0] * n_lat + a[1], b[0] * n_lat + b[1]))
    return pairs


def halos(x, flip):
    n_lon = lax.axis_size("lon")
    n_lat = lax.axis_size("lat")
    lon_i = lax.axis_index("lon")
    lat_j = lax.axis_index("lat")
    up = [(i, (i + 1) % n_lon) for i in range(n_lon)]
    down = [(b, a) for a, b in up]
    from_west = lax.ppermute(x[:, :, -1, :], "lon", up)
    from_east = lax.ppermute(x[:, :, 0, :], "lon", down)
    low = lon_i < n_lon // 2
    first_row = x[:, :, :, 0]
    last_row = x[:, :, :, -1]
    cw_pairs = ring_pairs(n_lon, n_lat)
    ccw_pairs = [(b, a) for a, b in cw_pairs]
    cw = lax.ppermute(jnp.where(low, last_row, first_row), ("lon", "lat"), cw_pairs)
    ccw = lax.ppermute(jnp.where(low, first_row, last_row), ("lon", "lat"), ccw_pairs)
    north_row = jnp.where(low, cw, ccw)
    south_row = jnp.where(low, ccw, cw)
    north_row = jnp.where(lat_j == 0, flip * north_row, north_row)
    south_row = jnp.where(lat_j == n_lat - 1, flip * south_row, south_row)
    return north_row, south_row, from_west, from_east


def shifted(x, halo):
    north_row, south_row, from_west, from_east = halo
    north = jnp.concatenate([north_row[..., None], x[..., :-1]], axis=3)
    south = jnp.concatenate([x[..., 1:], south_row[..., None]], axis=3)
    west = jnp.concatenate([from_west[:, :, None, :], x[:, :, :-1, :]], axis=2)
    east = jnp.concatenate([x[:, :, 1:, :], from_east[:, :, None, :]], axis=2)
    return north, south, west, east


def mix(coupling, v, transpose):
    out = []
    for g in range(v.shape[0]):
        acc = None
        for f in range(v.shape[0]):
            c = coupling[:, f, g] if transpose else coupling[:, g, f]
            term = c[:, None, None] * v[f]
            acc = term if acc is None else acc + term
        out.append(acc)
    return jnp.stack(out)


def edge_halos(first_col, last_col, first_row, last_row, flip):
    n_lon = lax.axis_size("lon")
    n_lat = lax.axis_size("lat")
    lon_i = lax.axis_index("lon")
    lat_j = lax.axis_index("lat")
    up = [(i, (i + 1) % n_lon) for i in range(n_lon)]
    down = [(b, a) for a, b in up]
    from_west = lax.ppermute(last_col, "lon", up)
    from_east = lax.ppermute(first_col, "lon", down)
    low = lon_i < n_lon // 2
    cw_pairs = ring_pairs(n_lon, n_lat)
    ccw_pairs = [(b, a) for a, b in cw_pairs]
    cw = lax.ppermute(jnp.where(low, last_row, first_row), ("lon", "lat"), cw_pairs)
    ccw = lax.ppermute(jnp.where(low, first_row, last_row), ("lon", "lat"), ccw_pairs)
    north_row = jnp.where(low, cw, ccw)
    south_row = jnp.where(low, ccw, cw)
    north_row = jnp.where(lat_j == 0, flip * north_row, north_row)
    south_row = jnp.where(lat_j == n_lat - 1, flip * south_row, south_row)
    return (north_row[..., None], south_row[..., None], from_west[:, :, None, :], from_east[:, :, None, :])


def neighbours_2d(v, hn, hs, hw, he):
    c_n, r_n = v.shape
    rows = lax.broadcasted_iota(jnp.int32, v.shape, 1)
    cols = lax.broadcasted_iota(jnp.int32, v.shape, 0)
    north = jnp.where(rows == 0, hn, pltpu.roll(v, 1, 1))
    south = jnp.where(rows == r_n - 1, hs, pltpu.roll(v, r_n - 1, 1))
    west = jnp.where(cols == 0, hw, pltpu.roll(v, 1, 0))
    east = jnp.where(cols == c_n - 1, he, pltpu.roll(v, c_n - 1, 0))
    return north, south, west, east


def write_edges(v, f, l, fc, lc, fr, lr):
    fc[f, l] = v[0:1, :]
    lc[f, l] = v[-1:, :]
    fr[f, l] = v[:, 0:1]
    lr[f, l] = v[:, -1:]


def forward_kernel(cpl, x_ref, c_ref, hn, hs, hw, he, xn_ref, d_ref, fc, lc, fr, lr):
    nf = x_ref.shape[0]

    def body(l, carry):
        xs = [x_ref[f, l] for f in range(nf)]
        cs = [c_ref[d, l] for d in range(4)]
        total = cs[0] + cs[1] + cs[2] + cs[3]
        for g in range(nf):
            v = xs[g]
            north, south, west, east = neighbours_2d(v, hn[g, l], hs[g, l], hw[g, l], he[g, l])
            mixed = cpl[l * nf * nf + g * nf] * xs[0]
            for f in range(1, nf):
                mixed = mixed + cpl[l * nf * nf + g * nf + f] * xs[f]
            y = v + cs[0] * north + cs[1] * south + cs[2] * west + cs[3] * east - total * v + 0.25 * mixed
            t = jnp.tanh(y)
            xn = y - 0.5 * t
            xn_ref[g, l] = xn
            d_ref[g, l] = 1.0 - 0.5 * (1.0 - t * t)
            write_edges(xn, g, l, fc, lc, fr, lr)
        return carry

    lax.fori_loop(0, x_ref.shape[1], body, 0)


def backward_kernel(cpl, ly_ref, c_ref, b_ref, dp_ref, hn, hs, hw, he, out_ref, fc, lc, fr, lr, *, last):
    nf = ly_ref.shape[0]

    def body(l, carry):
        ls = [ly_ref[f, l] for f in range(nf)]
        cs = [c_ref[d, l] for d in range(4)]
        total = cs[0] + cs[1] + cs[2] + cs[3]
        bs = [b_ref[d, l] for d in range(4)]
        for o in range(nf):
            v = ls[o]
            north, south, west, east = neighbours_2d(v, hn[o, l], hs[o, l], hw[o, l], he[o, l])
            back = cpl[l * nf * nf + o] * ls[0]
            for g in range(1, nf):
                back = back + cpl[l * nf * nf + g * nf + o] * ls[g]
            lam = v - total * v + 0.25 * back + bs[0] * north + bs[1] * south + bs[2] * west + bs[3] * east
            if last:
                out_ref[o, l] = lam
            else:
                nxt = lam * dp_ref[o, l]
                out_ref[o, l] = nxt
                write_edges(nxt, o, l, fc, lc, fr, lr)
        return carry

    lax.fori_loop(0, ly_ref.shape[1], body, 0)


def edge_shapes(x):
    f, l, c, r = x.shape
    return [
        jax.ShapeDtypeStruct((f, l, 1, r), x.dtype),
        jax.ShapeDtypeStruct((f, l, 1, r), x.dtype),
        jax.ShapeDtypeStruct((f, l, c, 1), x.dtype),
        jax.ShapeDtypeStruct((f, l, c, 1), x.dtype),
    ]


def vmem_specs(n):
    return [pl.BlockSpec(memory_space=pltpu.VMEM) for _ in range(n)]


def forward_step(cpl, x, coef, halo):
    outs = [jax.ShapeDtypeStruct(x.shape, x.dtype)] * 2 + edge_shapes(x)
    return pl.pallas_call(
        forward_kernel,
        out_shape=outs,
        in_specs=[pl.BlockSpec(memory_space=pltpu.SMEM)] + vmem_specs(6),
        out_specs=vmem_specs(6),
    )(cpl, x, coef, *halo)


def backward_step(cpl, ly, coef, back_coef, dprev, halo, last):
    outs = [jax.ShapeDtypeStruct(ly.shape, ly.dtype)] + edge_shapes(ly)
    return pl.pallas_call(
        lambda *refs: backward_kernel(*refs, last=last),
        out_shape=outs,
        in_specs=[pl.BlockSpec(memory_space=pltpu.SMEM)] + vmem_specs(8),
        out_specs=vmem_specs(5),
    )(cpl, ly, coef, back_coef, dprev, *halo)


def edges_of(x):
    return (x[:, :, 0, :], x[:, :, -1, :], x[:, :, :, 0], x[:, :, :, -1])


def squeezed(edges):
    fc, lc, fr, lr = edges
    return (fc[:, :, 0, :], lc[:, :, 0, :], fr[..., 0], lr[..., 0])


def on_device(
    initial_state, coefficients, coupling, obs_band, obs_cell, obs_value, obs_weight, obs_count
):
    wind_flip = jnp.array([-1.0, -1.0, 1.0, 1.0], dtype=jnp.float32).reshape(4, 1, 1)
    plain_flip = jnp.ones((4, 1, 1), jnp.float32)
    cpl = coupling.reshape(-1)
    factors = []
    x = initial_state
    edges = edges_of(x)
    for step in range(STEPS):
        x, dfac, *kernel_edges = forward_step(cpl, x, coefficients, edge_halos(*edges, wind_flip))
        factors.append(dfac)
        edges = squeezed(kernel_edges)

    n_lon = lax.axis_size("lon")
    rows = obs_cell.shape[1]
    band = obs_band[0, :, 0]
    valid = jnp.arange(rows, dtype=jnp.int32) < obs_count[0, 0]
    weight = jnp.where(valid, obs_weight[0], 0.0)
    ids = jnp.arange(rows, dtype=jnp.int32)
    same = (band[:, None] == band[None, :]) & (ids[None, :] < ids[:, None])
    rank = jnp.sum(same.astype(jnp.int32), axis=1)
    slot = band * CAP + rank
    payload = jnp.stack([obs_value[0], weight, obs_cell[0].astype(jnp.float32)], axis=1)
    slots = jnp.arange(n_lon * CAP, dtype=jnp.int32)
    hit = slot[None, :] == slots[:, None]
    send = jnp.sum(jnp.where(hit[:, :, None], payload[None, :, :], 0.0), axis=1)
    arrived = lax.all_to_all(send, "lon", 0, 0, tiled=True)
    values = arrived[:, 0]
    weights = arrived[:, 1]
    cells = arrived[:, 2].astype(jnp.int32)
    lanes = x.shape[3]
    row_of = cells // lanes
    lane_of = cells % lanes
    table = x.reshape(-1, lanes)
    lane_hit = lane_of[:, None] == jnp.arange(lanes, dtype=jnp.int32)[None, :]
    picked = jnp.sum(jnp.where(lane_hit, table[row_of], 0.0), axis=1)
    forcing = weights * (picked - values)
    spread = jnp.where(lane_hit, forcing[:, None], 0.0)
    lam = jnp.zeros_like(table).at[row_of].add(spread).reshape(x.shape)

    near_n, near_s, near_w, near_e = shifted(coefficients, halos(coefficients, plain_flip))
    row_ids = jnp.arange(coefficients.shape[3], dtype=jnp.int32)[None, :]
    polar_top = (lax.axis_index("lat") == 0) & (row_ids == 0)
    polar_bottom = (lax.axis_index("lat") == lax.axis_size("lat") - 1) & (
        row_ids == coefficients.shape[3] - 1
    )
    back_coef = jnp.stack([
        jnp.where(polar_top, near_n[0], near_n[1]),
        jnp.where(polar_bottom, near_s[1], near_s[0]),
        near_w[3],
        near_e[2],
    ])
    lam_y = lam * factors[STEPS - 1]
    edges = edges_of(lam_y)
    for step in range(STEPS - 1, -1, -1):
        last = step == 0
        dprev = factors[step - 1] if not last else factors[0]
        lam_y, *kernel_edges = backward_step(
            cpl, lam_y, coefficients, back_coef, dprev, edge_halos(*edges, wind_flip), last
        )
        edges = squeezed(kernel_edges)
    return (x, lam_y)


def solution(mesh):
    in_specs = (
        P(None, None, "lon", "lat"),
        P(None, None, "lon", "lat"),
        P(),
        P("lat", "lon", None),
        P("lat", "lon"),
        P("lat", "lon"),
        P("lat", "lon"),
        P("lat", "lon"),
    )
    out_specs = (P(None, None, "lon", "lat"), P(None, None, "lon", "lat"))
    return jax.shard_map(
        on_device, mesh=mesh, in_specs=in_specs, out_specs=out_specs, check_vma=False
    )
```

```python
import jax
import jax.numpy as jnp
from jax import lax
from jax.sharding import PartitionSpec as P
from jax.experimental import pallas as pl
from jax.experimental.pallas import tpu as pltpu

STEPS = 2
CAP = 32
UNROLL = 1


def ring_pairs(n_lon, n_lat):
    half = n_lon // 2
    pairs = []
    for i in range(half):
        ring = [(i, j) for j in range(n_lat)] + [(i + half, j) for j in range(n_lat - 1, -1, -1)]
        for k in range(len(ring)):
            a, b = ring[k], ring[(k + 1) % len(ring)]
            pairs.append((a[0] * n_lat + a[1], b[0] * n_lat + b[1]))
    return pairs


def halos(x, flip):
    n_lon = lax.axis_size("lon")
    n_lat = lax.axis_size("lat")
    lon_i = lax.axis_index("lon")
    lat_j = lax.axis_index("lat")
    up = [(i, (i + 1) % n_lon) for i in range(n_lon)]
    down = [(b, a) for a, b in up]
    from_west = lax.ppermute(x[:, :, -1, :], "lon", up)
    from_east = lax.ppermute(x[:, :, 0, :], "lon", down)
    low = lon_i < n_lon // 2
    first_row = x[:, :, :, 0]
    last_row = x[:, :, :, -1]
    cw_pairs = ring_pairs(n_lon, n_lat)
    ccw_pairs = [(b, a) for a, b in cw_pairs]
    cw = lax.ppermute(jnp.where(low, last_row, first_row), ("lon", "lat"), cw_pairs)
    ccw = lax.ppermute(jnp.where(low, first_row, last_row), ("lon", "lat"), ccw_pairs)
    north_row = jnp.where(low, cw, ccw)
    south_row = jnp.where(low, ccw, cw)
    north_row = jnp.where(lat_j == 0, flip * north_row, north_row)
    south_row = jnp.where(lat_j == n_lat - 1, flip * south_row, south_row)
    return north_row, south_row, from_west, from_east


def shifted(x, halo):
    north_row, south_row, from_west, from_east = halo
    north = jnp.concatenate([north_row[..., None], x[..., :-1]], axis=3)
    south = jnp.concatenate([x[..., 1:], south_row[..., None]], axis=3)
    west = jnp.concatenate([from_west[:, :, None, :], x[:, :, :-1, :]], axis=2)
    east = jnp.concatenate([x[:, :, 1:, :], from_east[:, :, None, :]], axis=2)
    return north, south, west, east


def mix(coupling, v, transpose):
    out = []
    for g in range(v.shape[0]):
        acc = None
        for f in range(v.shape[0]):
            c = coupling[:, f, g] if transpose else coupling[:, g, f]
            term = c[:, None, None] * v[f]
            acc = term if acc is None else acc + term
        out.append(acc)
    return jnp.stack(out)


def edge_halos(first_col, last_col, first_row, last_row, flip):
    n_lon = lax.axis_size("lon")
    n_lat = lax.axis_size("lat")
    lon_i = lax.axis_index("lon")
    lat_j = lax.axis_index("lat")
    up = [(i, (i + 1) % n_lon) for i in range(n_lon)]
    down = [(b, a) for a, b in up]
    from_west = lax.ppermute(last_col, "lon", up)
    from_east = lax.ppermute(first_col, "lon", down)
    low = lon_i < n_lon // 2
    cw_pairs = ring_pairs(n_lon, n_lat)
    ccw_pairs = [(b, a) for a, b in cw_pairs]
    cw = lax.ppermute(jnp.where(low, last_row, first_row), ("lon", "lat"), cw_pairs)
    ccw = lax.ppermute(jnp.where(low, first_row, last_row), ("lon", "lat"), ccw_pairs)
    north_row = jnp.where(low, cw, ccw)
    south_row = jnp.where(low, ccw, cw)
    north_row = jnp.where(lat_j == 0, flip * north_row, north_row)
    south_row = jnp.where(lat_j == n_lat - 1, flip * south_row, south_row)
    return (jnp.stack([north_row, south_row], axis=-1), from_west[:, :, None, :], from_east[:, :, None, :])


def edge_masks(shape):
    rows = lax.broadcasted_iota(jnp.int32, shape, 1)
    cols = lax.broadcasted_iota(jnp.int32, shape, 0)
    return rows == 0, rows == shape[1] - 1, cols == 0, cols == shape[0] - 1


def neighbours_2d(v, masks, hn, hs, hw, he):
    c_n, r_n = v.shape
    top, bottom, left, right = masks
    north = jnp.where(top, hn, pltpu.roll(v, 1, 1))
    south = jnp.where(bottom, hs, pltpu.roll(v, r_n - 1, 1))
    west = jnp.where(left, hw, pltpu.roll(v, 1, 0))
    east = jnp.where(right, he, pltpu.roll(v, c_n - 1, 0))
    return north, south, west, east


def write_edges(v, f, l, fc, lc, frl):
    fc[f, l] = v[0:1, :]
    lc[f, l] = v[-1:, :]
    frl[f, l, :, 0:1] = v[:, 0:1]
    frl[f, l, :, 1:2] = v[:, -1:]


def forward_kernel(cpl, x_ref, c_ref, hns, hw, he, xn_ref, d_ref, fc, lc, frl):
    nf = x_ref.shape[0]
    masks = edge_masks(x_ref.shape[2:])

    def body(l, carry):
        xs = [x_ref[f, l] for f in range(nf)]
        cs = [c_ref[d, l] for d in range(4)]
        total = cs[0] + cs[1] + cs[2] + cs[3]
        for g in range(nf):
            v = xs[g]
            north, south, west, east = neighbours_2d(v, masks, hns[g, l, :, 0:1], hns[g, l, :, 1:2], hw[g, l], he[g, l])
            mixed = cpl[l * nf * nf + g * nf] * xs[0]
            for f in range(1, nf):
                mixed = mixed + cpl[l * nf * nf + g * nf + f] * xs[f]
            y = v + cs[0] * north + cs[1] * south + cs[2] * west + cs[3] * east - total * v + 0.25 * mixed
            t = jnp.tanh(y)
            xn = y - 0.5 * t
            xn_ref[g, l] = xn
            d_ref[g, l] = 1.0 - 0.5 * (1.0 - t * t)
            write_edges(xn, g, l, fc, lc, frl)
        return carry

    lax.fori_loop(0, x_ref.shape[1], body, 0, unroll=UNROLL)


def backward_kernel(cpl, ly_ref, c_ref, b_ref, dp_ref, hns, hw, he, out_ref, fc, lc, frl, *, last):
    nf = ly_ref.shape[0]
    masks = edge_masks(ly_ref.shape[2:])

    def body(l, carry):
        ls = [ly_ref[f, l] for f in range(nf)]
        cs = [c_ref[d, l] for d in range(4)]
        total = cs[0] + cs[1] + cs[2] + cs[3]
        bs = [b_ref[d, l] for d in range(4)]
        for o in range(nf):
            v = ls[o]
            north, south, west, east = neighbours_2d(v, masks, hns[o, l, :, 0:1], hns[o, l, :, 1:2], hw[o, l], he[o, l])
            back = cpl[l * nf * nf + o] * ls[0]
            for g in range(1, nf):
                back = back + cpl[l * nf * nf + g * nf + o] * ls[g]
            lam = v - total * v + 0.25 * back + bs[0] * north + bs[1] * south + bs[2] * west + bs[3] * east
            if last:
                out_ref[o, l] = lam
            else:
                nxt = lam * dp_ref[o, l]
                out_ref[o, l] = nxt
                write_edges(nxt, o, l, fc, lc, frl)
        return carry

    lax.fori_loop(0, ly_ref.shape[1], body, 0, unroll=UNROLL)


def edge_shapes(x):
    f, l, c, r = x.shape
    return [
        jax.ShapeDtypeStruct((f, l, 1, r), x.dtype),
        jax.ShapeDtypeStruct((f, l, 1, r), x.dtype),
        jax.ShapeDtypeStruct((f, l, c, 2), x.dtype),
    ]


def vmem_specs(n):
    return [pl.BlockSpec(memory_space=pltpu.VMEM) for _ in range(n)]


def forward_step(cpl, x, coef, halo):
    outs = [jax.ShapeDtypeStruct(x.shape, x.dtype)] * 2 + edge_shapes(x)
    return pl.pallas_call(
        forward_kernel,
        out_shape=outs,
        in_specs=[pl.BlockSpec(memory_space=pltpu.SMEM)] + vmem_specs(5),
        out_specs=vmem_specs(5),
    )(cpl, x, coef, *halo)


def backward_step(cpl, ly, coef, back_coef, dprev, halo, last):
    outs = [jax.ShapeDtypeStruct(ly.shape, ly.dtype)] + edge_shapes(ly)
    return pl.pallas_call(
        lambda *refs: backward_kernel(*refs, last=last),
        out_shape=outs,
        in_specs=[pl.BlockSpec(memory_space=pltpu.SMEM)] + vmem_specs(7),
        out_specs=vmem_specs(4),
    )(cpl, ly, coef, back_coef, dprev, *halo)


def edges_of(x):
    return (x[:, :, 0, :], x[:, :, -1, :], x[:, :, :, 0], x[:, :, :, -1])


def squeezed(edges):
    fc, lc, frl = edges
    return (fc[:, :, 0, :], lc[:, :, 0, :], frl[..., 0], frl[..., 1])


def on_device(
    initial_state, coefficients, coupling, obs_band, obs_cell, obs_value, obs_weight, obs_count
):
    wind_flip = jnp.array([-1.0, -1.0, 1.0, 1.0], dtype=jnp.float32).reshape(4, 1, 1)
    plain_flip = jnp.ones((4, 1, 1), jnp.float32)
    cpl = coupling.reshape(-1)
    factors = []
    x = initial_state
    edges = edges_of(x)
    for step in range(STEPS):
        x, dfac, *kernel_edges = forward_step(cpl, x, coefficients, edge_halos(*edges, wind_flip))
        factors.append(dfac)
        edges = squeezed(kernel_edges)

    n_lon = lax.axis_size("lon")
    rows = obs_cell.shape[1]
    band = obs_band[0, :, 0]
    valid = jnp.arange(rows, dtype=jnp.int32) < obs_count[0, 0]
    weight = jnp.where(valid, obs_weight[0], 0.0)
    ids = jnp.arange(rows, dtype=jnp.int32)
    same = (band[:, None] == band[None, :]) & (ids[None, :] < ids[:, None])
    rank = jnp.sum(same.astype(jnp.int32), axis=1)
    slot = band * CAP + rank
    payload = jnp.stack([obs_value[0], weight, obs_cell[0].astype(jnp.float32)], axis=1)
    slots = jnp.arange(n_lon * CAP, dtype=jnp.int32)
    hit = slot[None, :] == slots[:, None]
    send = jnp.sum(jnp.where(hit[:, :, None], payload[None, :, :], 0.0), axis=1)
    arrived = lax.all_to_all(send, "lon", 0, 0, tiled=True)
    values = arrived[:, 0]
    weights = arrived[:, 1]
    cells = arrived[:, 2].astype(jnp.int32)
    lanes = x.shape[3]
    row_of = cells // lanes
    lane_of = cells % lanes
    table = x.reshape(-1, lanes)
    lane_hit = lane_of[:, None] == jnp.arange(lanes, dtype=jnp.int32)[None, :]
    picked = jnp.sum(jnp.where(lane_hit, table[row_of], 0.0), axis=1)
    forcing = weights * (picked - values)
    spread = jnp.where(lane_hit, forcing[:, None], 0.0)
    lam = jnp.zeros_like(table).at[row_of].add(spread).reshape(x.shape)

    near_n, near_s, near_w, near_e = shifted(coefficients, halos(coefficients, plain_flip))
    row_ids = jnp.arange(coefficients.shape[3], dtype=jnp.int32)[None, :]
    polar_top = (lax.axis_index("lat") == 0) & (row_ids == 0)
    polar_bottom = (lax.axis_index("lat") == lax.axis_size("lat") - 1) & (
        row_ids == coefficients.shape[3] - 1
    )
    back_coef = jnp.stack([
        jnp.where(polar_top, near_n[0], near_n[1]),
        jnp.where(polar_bottom, near_s[1], near_s[0]),
        near_w[3],
        near_e[2],
    ])
    lam_y = lam * factors[STEPS - 1]
    edges = edges_of(lam_y)
    for step in range(STEPS - 1, -1, -1):
        last = step == 0
        dprev = factors[step - 1] if not last else factors[0]
        lam_y, *kernel_edges = backward_step(
            cpl, lam_y, coefficients, back_coef, dprev, edge_halos(*edges, wind_flip), last
        )
        edges = squeezed(kernel_edges)
    return (x, lam_y)


def solution(mesh):
    in_specs = (
        P(None, None, "lon", "lat"),
        P(None, None, "lon", "lat"),
        P(),
        P("lat", "lon", None),
        P("lat", "lon"),
        P("lat", "lon"),
        P("lat", "lon"),
        P("lat", "lon"),
    )
    out_specs = (P(None, None, "lon", "lat"), P(None, None, "lon", "lat"))
    return jax.shard_map(
        on_device, mesh=mesh, in_specs=in_specs, out_specs=out_specs, check_vma=False
    )
```

```python
import jax
import jax.numpy as jnp
from jax import lax
from jax.sharding import PartitionSpec as P
from jax.experimental import pallas as pl
from jax.experimental.pallas import tpu as pltpu

STEPS = 2
CAP = 32
UNROLL = 1
LEVEL_BLOCK = 8


def ring_pairs(n_lon, n_lat):
    half = n_lon // 2
    pairs = []
    for i in range(half):
        ring = [(i, j) for j in range(n_lat)] + [(i + half, j) for j in range(n_lat - 1, -1, -1)]
        for k in range(len(ring)):
            a, b = ring[k], ring[(k + 1) % len(ring)]
            pairs.append((a[0] * n_lat + a[1], b[0] * n_lat + b[1]))
    return pairs


def halos(x, flip):
    n_lon = lax.axis_size("lon")
    n_lat = lax.axis_size("lat")
    lon_i = lax.axis_index("lon")
    lat_j = lax.axis_index("lat")
    up = [(i, (i + 1) % n_lon) for i in range(n_lon)]
    down = [(b, a) for a, b in up]
    from_west = lax.ppermute(x[:, :, -1, :], "lon", up)
    from_east = lax.ppermute(x[:, :, 0, :], "lon", down)
    low = lon_i < n_lon // 2
    first_row = x[:, :, :, 0]
    last_row = x[:, :, :, -1]
    cw_pairs = ring_pairs(n_lon, n_lat)
    ccw_pairs = [(b, a) for a, b in cw_pairs]
    cw = lax.ppermute(jnp.where(low, last_row, first_row), ("lon", "lat"), cw_pairs)
    ccw = lax.ppermute(jnp.where(low, first_row, last_row), ("lon", "lat"), ccw_pairs)
    north_row = jnp.where(low, cw, ccw)
    south_row = jnp.where(low, ccw, cw)
    north_row = jnp.where(lat_j == 0, flip * north_row, north_row)
    south_row = jnp.where(lat_j == n_lat - 1, flip * south_row, south_row)
    return north_row, south_row, from_west, from_east


def shifted(x, halo):
    north_row, south_row, from_west, from_east = halo
    north = jnp.concatenate([north_row[..., None], x[..., :-1]], axis=3)
    south = jnp.concatenate([x[..., 1:], south_row[..., None]], axis=3)
    west = jnp.concatenate([from_west[:, :, None, :], x[:, :, :-1, :]], axis=2)
    east = jnp.concatenate([x[:, :, 1:, :], from_east[:, :, None, :]], axis=2)
    return north, south, west, east


def mix(coupling, v, transpose):
    out = []
    for g in range(v.shape[0]):
        acc = None
        for f in range(v.shape[0]):
            c = coupling[:, f, g] if transpose else coupling[:, g, f]
            term = c[:, None, None] * v[f]
            acc = term if acc is None else acc + term
        out.append(acc)
    return jnp.stack(out)


def edge_halos(first_col, last_col, first_row, last_row, flip):
    n_lon = lax.axis_size("lon")
    n_lat = lax.axis_size("lat")
    lon_i = lax.axis_index("lon")
    lat_j = lax.axis_index("lat")
    up = [(i, (i + 1) % n_lon) for i in range(n_lon)]
    down = [(b, a) for a, b in up]
    from_west = lax.ppermute(last_col, "lon", up)
    from_east = lax.ppermute(first_col, "lon", down)
    low = lon_i < n_lon // 2
    cw_pairs = ring_pairs(n_lon, n_lat)
    ccw_pairs = [(b, a) for a, b in cw_pairs]
    cw = lax.ppermute(jnp.where(low, last_row, first_row), ("lon", "lat"), cw_pairs)
    ccw = lax.ppermute(jnp.where(low, first_row, last_row), ("lon", "lat"), ccw_pairs)
    north_row = jnp.where(low, cw, ccw)
    south_row = jnp.where(low, ccw, cw)
    north_row = jnp.where(lat_j == 0, flip * north_row, north_row)
    south_row = jnp.where(lat_j == n_lat - 1, flip * south_row, south_row)
    return (jnp.stack([north_row, south_row], axis=-1), from_west[:, :, None, :], from_east[:, :, None, :])


def edge_masks(shape):
    rows = lax.broadcasted_iota(jnp.int32, shape, 1)
    cols = lax.broadcasted_iota(jnp.int32, shape, 0)
    return rows == 0, rows == shape[1] - 1, cols == 0, cols == shape[0] - 1


def neighbours_2d(v, masks, hn, hs, hw, he):
    c_n, r_n = v.shape
    top, bottom, left, right = masks
    north = jnp.where(top, hn, pltpu.roll(v, 1, 1))
    south = jnp.where(bottom, hs, pltpu.roll(v, r_n - 1, 1))
    west = jnp.where(left, hw, pltpu.roll(v, 1, 0))
    east = jnp.where(right, he, pltpu.roll(v, c_n - 1, 0))
    return north, south, west, east


def write_edges(v, f, l, fc, lc, frl):
    fc[f, l] = v[0:1, :]
    lc[f, l] = v[-1:, :]
    frl[f, l, :, 0:1] = v[:, 0:1]
    frl[f, l, :, 1:2] = v[:, -1:]


def forward_kernel(cpl, x_ref, c_ref, hns, hw, he, xn_ref, d_ref, fc, lc, frl):
    nf = x_ref.shape[0]
    masks = edge_masks(x_ref.shape[2:])

    def body(l, carry):
        lev = pl.program_id(0) * x_ref.shape[1] + l
        xs = [x_ref[f, l] for f in range(nf)]
        cs = [c_ref[d, l] for d in range(4)]
        total = cs[0] + cs[1] + cs[2] + cs[3]
        for g in range(nf):
            v = xs[g]
            north, south, west, east = neighbours_2d(v, masks, hns[g, l, :, 0:1], hns[g, l, :, 1:2], hw[g, l], he[g, l])
            mixed = cpl[lev * nf * nf + g * nf] * xs[0]
            for f in range(1, nf):
                mixed = mixed + cpl[lev * nf * nf + g * nf + f] * xs[f]
            y = v + cs[0] * north + cs[1] * south + cs[2] * west + cs[3] * east - total * v + 0.25 * mixed
            t = jnp.tanh(y)
            xn = y - 0.5 * t
            xn_ref[g, l] = xn
            d_ref[g, l] = 1.0 - 0.5 * (1.0 - t * t)
            write_edges(xn, g, l, fc, lc, frl)
        return carry

    lax.fori_loop(0, x_ref.shape[1], body, 0, unroll=UNROLL)


def backward_kernel(cpl, ly_ref, c_ref, b_ref, dp_ref, hns, hw, he, out_ref, fc, lc, frl, *, last):
    nf = ly_ref.shape[0]
    masks = edge_masks(ly_ref.shape[2:])

    def body(l, carry):
        lev = pl.program_id(0) * ly_ref.shape[1] + l
        ls = [ly_ref[f, l] for f in range(nf)]
        cs = [c_ref[d, l] for d in range(4)]
        total = cs[0] + cs[1] + cs[2] + cs[3]
        bs = [b_ref[d, l] for d in range(4)]
        for o in range(nf):
            v = ls[o]
            north, south, west, east = neighbours_2d(v, masks, hns[o, l, :, 0:1], hns[o, l, :, 1:2], hw[o, l], he[o, l])
            back = cpl[lev * nf * nf + o] * ls[0]
            for g in range(1, nf):
                back = back + cpl[lev * nf * nf + g * nf + o] * ls[g]
            lam = v - total * v + 0.25 * back + bs[0] * north + bs[1] * south + bs[2] * west + bs[3] * east
            if last:
                out_ref[o, l] = lam
            else:
                nxt = lam * dp_ref[o, l]
                out_ref[o, l] = nxt
                write_edges(nxt, o, l, fc, lc, frl)
        return carry

    lax.fori_loop(0, ly_ref.shape[1], body, 0, unroll=UNROLL)


def edge_shapes(x):
    f, l, c, r = x.shape
    return [
        jax.ShapeDtypeStruct((f, l, 1, r), x.dtype),
        jax.ShapeDtypeStruct((f, l, 1, r), x.dtype),
        jax.ShapeDtypeStruct((f, l, c, 2), x.dtype),
    ]


def level_specs(arrays):
    specs = []
    for a in arrays:
        block = (a.shape[0], LEVEL_BLOCK) + tuple(a.shape[2:])
        specs.append(pl.BlockSpec(block, lambda i: (0, i, 0, 0)))
    return specs


def forward_step(cpl, x, coef, halo):
    outs = [jax.ShapeDtypeStruct(x.shape, x.dtype)] * 2 + edge_shapes(x)
    ins = [x, coef, *halo]
    return pl.pallas_call(
        forward_kernel,
        out_shape=outs,
        grid=(x.shape[1] // LEVEL_BLOCK,),
        in_specs=[pl.BlockSpec(memory_space=pltpu.SMEM)] + level_specs(ins),
        out_specs=level_specs(outs),
    )(cpl, *ins)


def backward_step(cpl, ly, coef, back_coef, dprev, halo, last):
    outs = [jax.ShapeDtypeStruct(ly.shape, ly.dtype)] + edge_shapes(ly)
    ins = [ly, coef, back_coef, dprev, *halo]
    return pl.pallas_call(
        lambda *refs: backward_kernel(*refs, last=last),
        out_shape=outs,
        grid=(ly.shape[1] // LEVEL_BLOCK,),
        in_specs=[pl.BlockSpec(memory_space=pltpu.SMEM)] + level_specs(ins),
        out_specs=level_specs(outs),
    )(cpl, *ins)


def edges_of(x):
    return (x[:, :, 0, :], x[:, :, -1, :], x[:, :, :, 0], x[:, :, :, -1])


def squeezed(edges):
    fc, lc, frl = edges
    return (fc[:, :, 0, :], lc[:, :, 0, :], frl[..., 0], frl[..., 1])


def on_device(
    initial_state, coefficients, coupling, obs_band, obs_cell, obs_value, obs_weight, obs_count
):
    wind_flip = jnp.array([-1.0, -1.0, 1.0, 1.0], dtype=jnp.float32).reshape(4, 1, 1)
    plain_flip = jnp.ones((4, 1, 1), jnp.float32)
    cpl = coupling.reshape(-1)
    factors = []
    x = initial_state
    edges = edges_of(x)
    for step in range(STEPS):
        x, dfac, *kernel_edges = forward_step(cpl, x, coefficients, edge_halos(*edges, wind_flip))
        factors.append(dfac)
        edges = squeezed(kernel_edges)

    n_lon = lax.axis_size("lon")
    rows = obs_cell.shape[1]
    band = obs_band[0, :, 0]
    valid = jnp.arange(rows, dtype=jnp.int32) < obs_count[0, 0]
    weight = jnp.where(valid, obs_weight[0], 0.0)
    ids = jnp.arange(rows, dtype=jnp.int32)
    same = (band[:, None] == band[None, :]) & (ids[None, :] < ids[:, None])
    rank = jnp.sum(same.astype(jnp.int32), axis=1)
    slot = band * CAP + rank
    payload = jnp.stack([obs_value[0], weight, obs_cell[0].astype(jnp.float32)], axis=1)
    slots = jnp.arange(n_lon * CAP, dtype=jnp.int32)
    hit = slot[None, :] == slots[:, None]
    send = jnp.sum(jnp.where(hit[:, :, None], payload[None, :, :], 0.0), axis=1)
    arrived = lax.all_to_all(send, "lon", 0, 0, tiled=True)
    values = arrived[:, 0]
    weights = arrived[:, 1]
    cells = arrived[:, 2].astype(jnp.int32)
    lanes = x.shape[3]
    row_of = cells // lanes
    lane_of = cells % lanes
    table = x.reshape(-1, lanes)
    lane_hit = lane_of[:, None] == jnp.arange(lanes, dtype=jnp.int32)[None, :]
    picked = jnp.sum(jnp.where(lane_hit, table[row_of], 0.0), axis=1)
    forcing = weights * (picked - values)
    spread = jnp.where(lane_hit, forcing[:, None], 0.0)
    lam = jnp.zeros_like(table).at[row_of].add(spread).reshape(x.shape)

    near_n, near_s, near_w, near_e = shifted(coefficients, halos(coefficients, plain_flip))
    row_ids = jnp.arange(coefficients.shape[3], dtype=jnp.int32)[None, :]
    polar_top = (lax.axis_index("lat") == 0) & (row_ids == 0)
    polar_bottom = (lax.axis_index("lat") == lax.axis_size("lat") - 1) & (
        row_ids == coefficients.shape[3] - 1
    )
    back_coef = jnp.stack([
        jnp.where(polar_top, near_n[0], near_n[1]),
        jnp.where(polar_bottom, near_s[1], near_s[0]),
        near_w[3],
        near_e[2],
    ])
    lam_y = lam * factors[STEPS - 1]
    edges = edges_of(lam_y)
    for step in range(STEPS - 1, -1, -1):
        last = step == 0
        dprev = factors[step - 1] if not last else factors[0]
        lam_y, *kernel_edges = backward_step(
            cpl, lam_y, coefficients, back_coef, dprev, edge_halos(*edges, wind_flip), last
        )
        edges = squeezed(kernel_edges)
    return (x, lam_y)


def solution(mesh):
    in_specs = (
        P(None, None, "lon", "lat"),
        P(None, None, "lon", "lat"),
        P(),
        P("lat", "lon", None),
        P("lat", "lon"),
        P("lat", "lon"),
        P("lat", "lon"),
        P("lat", "lon"),
    )
    out_specs = (P(None, None, "lon", "lat"), P(None, None, "lon", "lat"))
    return jax.shard_map(
        on_device, mesh=mesh, in_specs=in_specs, out_specs=out_specs, check_vma=False
    )
```

```python
import jax
import jax.numpy as jnp
from jax import lax
from jax.sharding import PartitionSpec as P
from jax.experimental import pallas as pl
from jax.experimental.pallas import tpu as pltpu

STEPS = 2
CAP = 32
UNROLL = 1
LEVEL_BLOCK = 8


def ring_pairs(n_lon, n_lat):
    half = n_lon // 2
    pairs = []
    for i in range(half):
        ring = [(i, j) for j in range(n_lat)] + [(i + half, j) for j in range(n_lat - 1, -1, -1)]
        for k in range(len(ring)):
            a, b = ring[k], ring[(k + 1) % len(ring)]
            pairs.append((a[0] * n_lat + a[1], b[0] * n_lat + b[1]))
    return pairs


def halos(x, flip):
    n_lon = lax.axis_size("lon")
    n_lat = lax.axis_size("lat")
    lon_i = lax.axis_index("lon")
    lat_j = lax.axis_index("lat")
    up = [(i, (i + 1) % n_lon) for i in range(n_lon)]
    down = [(b, a) for a, b in up]
    from_west = lax.ppermute(x[:, :, -1, :], "lon", up)
    from_east = lax.ppermute(x[:, :, 0, :], "lon", down)
    low = lon_i < n_lon // 2
    first_row = x[:, :, :, 0]
    last_row = x[:, :, :, -1]
    cw_pairs = ring_pairs(n_lon, n_lat)
    ccw_pairs = [(b, a) for a, b in cw_pairs]
    cw = lax.ppermute(jnp.where(low, last_row, first_row), ("lon", "lat"), cw_pairs)
    ccw = lax.ppermute(jnp.where(low, first_row, last_row), ("lon", "lat"), ccw_pairs)
    north_row = jnp.where(low, cw, ccw)
    south_row = jnp.where(low, ccw, cw)
    north_row = jnp.where(lat_j == 0, flip * north_row, north_row)
    south_row = jnp.where(lat_j == n_lat - 1, flip * south_row, south_row)
    return north_row, south_row, from_west, from_east


def shifted(x, halo):
    north_row, south_row, from_west, from_east = halo
    north = jnp.concatenate([north_row[..., None], x[..., :-1]], axis=3)
    south = jnp.concatenate([x[..., 1:], south_row[..., None]], axis=3)
    west = jnp.concatenate([from_west[:, :, None, :], x[:, :, :-1, :]], axis=2)
    east = jnp.concatenate([x[:, :, 1:, :], from_east[:, :, None, :]], axis=2)
    return north, south, west, east


def mix(coupling, v, transpose):
    out = []
    for g in range(v.shape[0]):
        acc = None
        for f in range(v.shape[0]):
            c = coupling[:, f, g] if transpose else coupling[:, g, f]
            term = c[:, None, None] * v[f]
            acc = term if acc is None else acc + term
        out.append(acc)
    return jnp.stack(out)


def edge_halos(first_col, last_col, first_row, last_row, flip):
    n_lon = lax.axis_size("lon")
    n_lat = lax.axis_size("lat")
    lon_i = lax.axis_index("lon")
    lat_j = lax.axis_index("lat")
    up = [(i, (i + 1) % n_lon) for i in range(n_lon)]
    down = [(b, a) for a, b in up]
    from_west = lax.ppermute(last_col, "lon", up)
    from_east = lax.ppermute(first_col, "lon", down)
    low = lon_i < n_lon // 2
    cw_pairs = ring_pairs(n_lon, n_lat)
    ccw_pairs = [(b, a) for a, b in cw_pairs]
    cw = lax.ppermute(jnp.where(low, last_row, first_row), ("lon", "lat"), cw_pairs)
    ccw = lax.ppermute(jnp.where(low, first_row, last_row), ("lon", "lat"), ccw_pairs)
    north_row = jnp.where(low, cw, ccw)
    south_row = jnp.where(low, ccw, cw)
    north_row = jnp.where(lat_j == 0, flip * north_row, north_row)
    south_row = jnp.where(lat_j == n_lat - 1, flip * south_row, south_row)
    return (jnp.stack([north_row, south_row], axis=-1), from_west, from_east)


def edge_masks(shape):
    rows = lax.broadcasted_iota(jnp.int32, shape, 1)
    cols = lax.broadcasted_iota(jnp.int32, shape, 0)
    return rows == 0, rows == shape[1] - 1, cols == 0, cols == shape[0] - 1


def neighbours_2d(v, masks, hn, hs, hw, he):
    c_n, r_n = v.shape
    top, bottom, left, right = masks
    north = jnp.where(top, hn, pltpu.roll(v, 1, 1))
    south = jnp.where(bottom, hs, pltpu.roll(v, r_n - 1, 1))
    west = jnp.where(left, hw, pltpu.roll(v, 1, 0))
    east = jnp.where(right, he, pltpu.roll(v, c_n - 1, 0))
    return north, south, west, east


def write_edges(v, f, l, fc, lc, frl):
    fc[f, pl.ds(l, 1), :] = v[0:1, :]
    lc[f, pl.ds(l, 1), :] = v[-1:, :]
    frl[f, l, :, 0:1] = v[:, 0:1]
    frl[f, l, :, 1:2] = v[:, -1:]


def forward_kernel(cpl, x_ref, c_ref, hns, hw, he, xn_ref, d_ref, fc, lc, frl):
    nf = x_ref.shape[0]
    masks = edge_masks(x_ref.shape[2:])

    def body(l, carry):
        lev = pl.program_id(0) * x_ref.shape[1] + l
        xs = [x_ref[f, l] for f in range(nf)]
        cs = [c_ref[d, l] for d in range(4)]
        total = cs[0] + cs[1] + cs[2] + cs[3]
        for g in range(nf):
            v = xs[g]
            north, south, west, east = neighbours_2d(v, masks, hns[g, l, :, 0:1], hns[g, l, :, 1:2], hw[g, pl.ds(l, 1), :], he[g, pl.ds(l, 1), :])
            mixed = cpl[lev * nf * nf + g * nf] * xs[0]
            for f in range(1, nf):
                mixed = mixed + cpl[lev * nf * nf + g * nf + f] * xs[f]
            y = v + cs[0] * north + cs[1] * south + cs[2] * west + cs[3] * east - total * v + 0.25 * mixed
            t = jnp.tanh(y)
            xn = y - 0.5 * t
            xn_ref[g, l] = xn
            d_ref[g, l] = 1.0 - 0.5 * (1.0 - t * t)
            write_edges(xn, g, l, fc, lc, frl)
        return carry

    lax.fori_loop(0, x_ref.shape[1], body, 0, unroll=UNROLL)


def backward_kernel(cpl, ly_ref, c_ref, b_ref, dp_ref, hns, hw, he, out_ref, fc, lc, frl, *, last):
    nf = ly_ref.shape[0]
    masks = edge_masks(ly_ref.shape[2:])

    def body(l, carry):
        lev = pl.program_id(0) * ly_ref.shape[1] + l
        ls = [ly_ref[f, l] for f in range(nf)]
        cs = [c_ref[d, l] for d in range(4)]
        total = cs[0] + cs[1] + cs[2] + cs[3]
        bs = [b_ref[d, l] for d in range(4)]
        for o in range(nf):
            v = ls[o]
            north, south, west, east = neighbours_2d(v, masks, hns[o, l, :, 0:1], hns[o, l, :, 1:2], hw[o, pl.ds(l, 1), :], he[o, pl.ds(l, 1), :])
            back = cpl[lev * nf * nf + o] * ls[0]
            for g in range(1, nf):
                back = back + cpl[lev * nf * nf + g * nf + o] * ls[g]
            lam = v - total * v + 0.25 * back + bs[0] * north + bs[1] * south + bs[2] * west + bs[3] * east
            if last:
                out_ref[o, l] = lam
            else:
                nxt = lam * dp_ref[o, l]
                out_ref[o, l] = nxt
                write_edges(nxt, o, l, fc, lc, frl)
        return carry

    lax.fori_loop(0, ly_ref.shape[1], body, 0, unroll=UNROLL)


def edge_shapes(x):
    f, l, c, r = x.shape
    return [
        jax.ShapeDtypeStruct((f, l, r), x.dtype),
        jax.ShapeDtypeStruct((f, l, r), x.dtype),
        jax.ShapeDtypeStruct((f, l, c, 2), x.dtype),
    ]


def level_specs(arrays):
    specs = []
    for a in arrays:
        block = (a.shape[0], LEVEL_BLOCK) + tuple(a.shape[2:])
        specs.append(pl.BlockSpec(block, lambda i, n=len(block): (0, i) + (0,) * (n - 2)))
    return specs


def forward_step(cpl, x, coef, halo):
    outs = [jax.ShapeDtypeStruct(x.shape, x.dtype)] * 2 + edge_shapes(x)
    ins = [x, coef, *halo]
    return pl.pallas_call(
        forward_kernel,
        out_shape=outs,
        grid=(x.shape[1] // LEVEL_BLOCK,),
        in_specs=[pl.BlockSpec(memory_space=pltpu.SMEM)] + level_specs(ins),
        out_specs=level_specs(outs),
    )(cpl, *ins)


def backward_step(cpl, ly, coef, back_coef, dprev, halo, last):
    outs = [jax.ShapeDtypeStruct(ly.shape, ly.dtype)] + edge_shapes(ly)
    ins = [ly, coef, back_coef, dprev, *halo]
    return pl.pallas_call(
        lambda *refs: backward_kernel(*refs, last=last),
        out_shape=outs,
        grid=(ly.shape[1] // LEVEL_BLOCK,),
        in_specs=[pl.BlockSpec(memory_space=pltpu.SMEM)] + level_specs(ins),
        out_specs=level_specs(outs),
    )(cpl, *ins)


def edges_of(x):
    return (x[:, :, 0, :], x[:, :, -1, :], x[:, :, :, 0], x[:, :, :, -1])


def squeezed(edges):
    fc, lc, frl = edges
    return (fc, lc, frl[..., 0], frl[..., 1])


def on_device(
    initial_state, coefficients, coupling, obs_band, obs_cell, obs_value, obs_weight, obs_count
):
    wind_flip = jnp.array([-1.0, -1.0, 1.0, 1.0], dtype=jnp.float32).reshape(4, 1, 1)
    plain_flip = jnp.ones((4, 1, 1), jnp.float32)
    cpl = coupling.reshape(-1)
    factors = []
    x = initial_state
    edges = edges_of(x)
    for step in range(STEPS):
        x, dfac, *kernel_edges = forward_step(cpl, x, coefficients, edge_halos(*edges, wind_flip))
        factors.append(dfac)
        edges = squeezed(kernel_edges)

    n_lon = lax.axis_size("lon")
    rows = obs_cell.shape[1]
    band = obs_band[0, :, 0]
    valid = jnp.arange(rows, dtype=jnp.int32) < obs_count[0, 0]
    weight = jnp.where(valid, obs_weight[0], 0.0)
    ids = jnp.arange(rows, dtype=jnp.int32)
    same = (band[:, None] == band[None, :]) & (ids[None, :] < ids[:, None])
    rank = jnp.sum(same.astype(jnp.int32), axis=1)
    slot = band * CAP + rank
    payload = jnp.stack([obs_value[0], weight, obs_cell[0].astype(jnp.float32)], axis=1)
    slots = jnp.arange(n_lon * CAP, dtype=jnp.int32)
    hit = slot[None, :] == slots[:, None]
    send = jnp.sum(jnp.where(hit[:, :, None], payload[None, :, :], 0.0), axis=1)
    arrived = lax.all_to_all(send, "lon", 0, 0, tiled=True)
    values = arrived[:, 0]
    weights = arrived[:, 1]
    cells = arrived[:, 2].astype(jnp.int32)
    lanes = x.shape[3]
    row_of = cells // lanes
    lane_of = cells % lanes
    lane_hit = lane_of[:, None] == jnp.arange(lanes, dtype=jnp.int32)[None, :]
    spread = jnp.concatenate(
        [jnp.where(lane_hit, weights[:, None], 0.0), jnp.where(lane_hit, (weights * values)[:, None], 0.0)],
        axis=1,
    )
    sums = jnp.zeros((x.size // lanes, 2 * lanes), x.dtype).at[row_of].add(spread)
    weight_sum = sums[:, :lanes].reshape(x.shape)
    weighted_values = sums[:, lanes:].reshape(x.shape)
    lam = x * weight_sum - weighted_values

    near_n, near_s, near_w, near_e = shifted(coefficients, halos(coefficients, plain_flip))
    row_ids = jnp.arange(coefficients.shape[3], dtype=jnp.int32)[None, :]
    polar_top = (lax.axis_index("lat") == 0) & (row_ids == 0)
    polar_bottom = (lax.axis_index("lat") == lax.axis_size("lat") - 1) & (
        row_ids == coefficients.shape[3] - 1
    )
    back_coef = jnp.stack([
        jnp.where(polar_top, near_n[0], near_n[1]),
        jnp.where(polar_bottom, near_s[1], near_s[0]),
        near_w[3],
        near_e[2],
    ])
    lam_y = lam * factors[STEPS - 1]
    edges = edges_of(lam_y)
    for step in range(STEPS - 1, -1, -1):
        last = step == 0
        dprev = factors[step - 1] if not last else factors[0]
        lam_y, *kernel_edges = backward_step(
            cpl, lam_y, coefficients, back_coef, dprev, edge_halos(*edges, wind_flip), last
        )
        edges = squeezed(kernel_edges)
    return (x, lam_y)


def solution(mesh):
    in_specs = (
        P(None, None, "lon", "lat"),
        P(None, None, "lon", "lat"),
        P(),
        P("lat", "lon", None),
        P("lat", "lon"),
        P("lat", "lon"),
        P("lat", "lon"),
        P("lat", "lon"),
    )
    out_specs = (P(None, None, "lon", "lat"), P(None, None, "lon", "lat"))
    return jax.shard_map(
        on_device, mesh=mesh, in_specs=in_specs, out_specs=out_specs, check_vma=False
    )
```

```python
import jax
import jax.numpy as jnp
from jax import lax
from jax.sharding import PartitionSpec as P
from jax.experimental import pallas as pl
from jax.experimental.pallas import tpu as pltpu

STEPS = 2
CAP = 32
UNROLL = 1
LEVEL_BLOCK = 8


def ring_pairs(n_lon, n_lat):
    half = n_lon // 2
    pairs = []
    for i in range(half):
        ring = [(i, j) for j in range(n_lat)] + [(i + half, j) for j in range(n_lat - 1, -1, -1)]
        for k in range(len(ring)):
            a, b = ring[k], ring[(k + 1) % len(ring)]
            pairs.append((a[0] * n_lat + a[1], b[0] * n_lat + b[1]))
    return pairs


def halos(x, flip):
    n_lon = lax.axis_size("lon")
    n_lat = lax.axis_size("lat")
    lon_i = lax.axis_index("lon")
    lat_j = lax.axis_index("lat")
    up = [(i, (i + 1) % n_lon) for i in range(n_lon)]
    down = [(b, a) for a, b in up]
    from_west = lax.ppermute(x[:, :, -1, :], "lon", up)
    from_east = lax.ppermute(x[:, :, 0, :], "lon", down)
    low = lon_i < n_lon // 2
    first_row = x[:, :, :, 0]
    last_row = x[:, :, :, -1]
    cw_pairs = ring_pairs(n_lon, n_lat)
    ccw_pairs = [(b, a) for a, b in cw_pairs]
    cw = lax.ppermute(jnp.where(low, last_row, first_row), ("lon", "lat"), cw_pairs)
    ccw = lax.ppermute(jnp.where(low, first_row, last_row), ("lon", "lat"), ccw_pairs)
    north_row = jnp.where(low, cw, ccw)
    south_row = jnp.where(low, ccw, cw)
    north_row = jnp.where(lat_j == 0, flip * north_row, north_row)
    south_row = jnp.where(lat_j == n_lat - 1, flip * south_row, south_row)
    return north_row, south_row, from_west, from_east


def shifted(x, halo):
    north_row, south_row, from_west, from_east = halo
    north = jnp.concatenate([north_row[..., None], x[..., :-1]], axis=3)
    south = jnp.concatenate([x[..., 1:], south_row[..., None]], axis=3)
    west = jnp.concatenate([from_west[:, :, None, :], x[:, :, :-1, :]], axis=2)
    east = jnp.concatenate([x[:, :, 1:, :], from_east[:, :, None, :]], axis=2)
    return north, south, west, east


def mix(coupling, v, transpose):
    out = []
    for g in range(v.shape[0]):
        acc = None
        for f in range(v.shape[0]):
            c = coupling[:, f, g] if transpose else coupling[:, g, f]
            term = c[:, None, None] * v[f]
            acc = term if acc is None else acc + term
        out.append(acc)
    return jnp.stack(out)


def edge_halos(first_col, last_col, first_row, last_row, flip):
    n_lon = lax.axis_size("lon")
    n_lat = lax.axis_size("lat")
    lon_i = lax.axis_index("lon")
    lat_j = lax.axis_index("lat")
    up = [(i, (i + 1) % n_lon) for i in range(n_lon)]
    down = [(b, a) for a, b in up]
    from_west = lax.ppermute(last_col, "lon", up)
    from_east = lax.ppermute(first_col, "lon", down)
    low = lon_i < n_lon // 2
    cw_pairs = ring_pairs(n_lon, n_lat)
    ccw_pairs = [(b, a) for a, b in cw_pairs]
    cw = lax.ppermute(jnp.where(low, last_row, first_row), ("lon", "lat"), cw_pairs)
    ccw = lax.ppermute(jnp.where(low, first_row, last_row), ("lon", "lat"), ccw_pairs)
    north_row = jnp.where(low, cw, ccw)
    south_row = jnp.where(low, ccw, cw)
    north_row = jnp.where(lat_j == 0, flip * north_row, north_row)
    south_row = jnp.where(lat_j == n_lat - 1, flip * south_row, south_row)
    return (jnp.stack([north_row, south_row], axis=-1), from_west[:, :, None, :], from_east[:, :, None, :])


def edge_masks(shape):
    rows = lax.broadcasted_iota(jnp.int32, shape, 1)
    cols = lax.broadcasted_iota(jnp.int32, shape, 0)
    return rows == 0, rows == shape[1] - 1, cols == 0, cols == shape[0] - 1


def neighbours_2d(v, masks, hn, hs, hw, he):
    c_n, r_n = v.shape
    top, bottom, left, right = masks
    north = jnp.where(top, hn, pltpu.roll(v, 1, 1))
    south = jnp.where(bottom, hs, pltpu.roll(v, r_n - 1, 1))
    west = jnp.where(left, hw, pltpu.roll(v, 1, 0))
    east = jnp.where(right, he, pltpu.roll(v, c_n - 1, 0))
    return north, south, west, east


def write_edges(v, f, l, fc, lc, frl):
    fc[f, l] = v[0:1, :]
    lc[f, l] = v[-1:, :]
    frl[f, l, :, 0:1] = v[:, 0:1]
    frl[f, l, :, 1:2] = v[:, -1:]


def forward_kernel(cpl, x_ref, c_ref, hns, hw, he, xn_ref, d_ref, fc, lc, frl):
    nf = x_ref.shape[0]
    masks = edge_masks(x_ref.shape[2:])

    def body(l, carry):
        lev = pl.program_id(0) * x_ref.shape[1] + l
        xs = [x_ref[f, l] for f in range(nf)]
        cs = [c_ref[d, l] for d in range(4)]
        total = cs[0] + cs[1] + cs[2] + cs[3]
        for g in range(nf):
            v = xs[g]
            north, south, west, east = neighbours_2d(v, masks, hns[g, l, :, 0:1], hns[g, l, :, 1:2], hw[g, l], he[g, l])
            mixed = cpl[lev * nf * nf + g * nf] * xs[0]
            for f in range(1, nf):
                mixed = mixed + cpl[lev * nf * nf + g * nf + f] * xs[f]
            y = v + cs[0] * north + cs[1] * south + cs[2] * west + cs[3] * east - total * v + 0.25 * mixed
            t = jnp.tanh(y)
            xn = y - 0.5 * t
            xn_ref[g, l] = xn
            d_ref[g, l] = 1.0 - 0.5 * (1.0 - t * t)
            write_edges(xn, g, l, fc, lc, frl)
        return carry

    lax.fori_loop(0, x_ref.shape[1], body, 0, unroll=UNROLL)


def backward_kernel(cpl, ly_ref, c_ref, b_ref, dp_ref, hns, hw, he, out_ref, fc, lc, frl, *, last):
    nf = ly_ref.shape[0]
    masks = edge_masks(ly_ref.shape[2:])

    def body(l, carry):
        lev = pl.program_id(0) * ly_ref.shape[1] + l
        ls = [ly_ref[f, l] for f in range(nf)]
        cs = [c_ref[d, l] for d in range(4)]
        total = cs[0] + cs[1] + cs[2] + cs[3]
        bs = [b_ref[d, l] for d in range(4)]
        for o in range(nf):
            v = ls[o]
            north, south, west, east = neighbours_2d(v, masks, hns[o, l, :, 0:1], hns[o, l, :, 1:2], hw[o, l], he[o, l])
            back = cpl[lev * nf * nf + o] * ls[0]
            for g in range(1, nf):
                back = back + cpl[lev * nf * nf + g * nf + o] * ls[g]
            lam = v - total * v + 0.25 * back + bs[0] * north + bs[1] * south + bs[2] * west + bs[3] * east
            if last:
                out_ref[o, l] = lam
            else:
                nxt = lam * dp_ref[o, l]
                out_ref[o, l] = nxt
                write_edges(nxt, o, l, fc, lc, frl)
        return carry

    lax.fori_loop(0, ly_ref.shape[1], body, 0, unroll=UNROLL)


def edge_shapes(x):
    f, l, c, r = x.shape
    return [
        jax.ShapeDtypeStruct((f, l, 1, r), x.dtype),
        jax.ShapeDtypeStruct((f, l, 1, r), x.dtype),
        jax.ShapeDtypeStruct((f, l, c, 2), x.dtype),
    ]


def level_specs(arrays):
    specs = []
    for a in arrays:
        block = (a.shape[0], LEVEL_BLOCK) + tuple(a.shape[2:])
        specs.append(pl.BlockSpec(block, lambda i: (0, i, 0, 0)))
    return specs


def forward_step(cpl, x, coef, halo):
    outs = [jax.ShapeDtypeStruct(x.shape, x.dtype)] * 2 + edge_shapes(x)
    ins = [x, coef, *halo]
    return pl.pallas_call(
        forward_kernel,
        out_shape=outs,
        grid=(x.shape[1] // LEVEL_BLOCK,),
        in_specs=[pl.BlockSpec(memory_space=pltpu.SMEM)] + level_specs(ins),
        out_specs=level_specs(outs),
    )(cpl, *ins)


def backward_step(cpl, ly, coef, back_coef, dprev, halo, last):
    outs = [jax.ShapeDtypeStruct(ly.shape, ly.dtype)] + edge_shapes(ly)
    ins = [ly, coef, back_coef, dprev, *halo]
    return pl.pallas_call(
        lambda *refs: backward_kernel(*refs, last=last),
        out_shape=outs,
        grid=(ly.shape[1] // LEVEL_BLOCK,),
        in_specs=[pl.BlockSpec(memory_space=pltpu.SMEM)] + level_specs(ins),
        out_specs=level_specs(outs),
    )(cpl, *ins)


def coef_kernel(flags, c_ref, hns, hw, he, out_ref):
    masks = edge_masks(c_ref.shape[2:])
    top, bottom = masks[0], masks[1]
    polar_top = jnp.logical_and(top, jnp.full(top.shape, flags[0], jnp.int32) == 1)
    polar_bottom = jnp.logical_and(bottom, jnp.full(bottom.shape, flags[1], jnp.int32) == 1)

    def body(l, carry):
        near = [neighbours_2d(c_ref[d, l], masks, hns[d, l, :, 0:1], hns[d, l, :, 1:2], hw[d, l], he[d, l]) for d in range(4)]
        out_ref[0, l] = jnp.where(polar_top, near[0][0], near[1][0])
        out_ref[1, l] = jnp.where(polar_bottom, near[1][1], near[0][1])
        out_ref[2, l] = near[3][2]
        out_ref[3, l] = near[2][3]
        return carry

    lax.fori_loop(0, c_ref.shape[1], body, 0, unroll=UNROLL)


def coef_neighbours(coef, halo):
    lat_j = lax.axis_index("lat")
    flags = jnp.stack([lat_j == 0, lat_j == lax.axis_size("lat") - 1]).astype(jnp.int32)
    ins = [coef, *halo]
    return pl.pallas_call(
        coef_kernel,
        out_shape=jax.ShapeDtypeStruct(coef.shape, coef.dtype),
        grid=(coef.shape[1] // LEVEL_BLOCK,),
        in_specs=[pl.BlockSpec(memory_space=pltpu.SMEM)] + level_specs(ins),
        out_specs=level_specs([coef])[0],
    )(flags, *ins)


def edges_of(x):
    return (x[:, :, 0, :], x[:, :, -1, :], x[:, :, :, 0], x[:, :, :, -1])


def squeezed(edges):
    fc, lc, frl = edges
    return (fc[:, :, 0, :], lc[:, :, 0, :], frl[..., 0], frl[..., 1])


def on_device(
    initial_state, coefficients, coupling, obs_band, obs_cell, obs_value, obs_weight, obs_count
):
    wind_flip = jnp.array([-1.0, -1.0, 1.0, 1.0], dtype=jnp.float32).reshape(4, 1, 1)
    plain_flip = jnp.ones((4, 1, 1), jnp.float32)
    cpl = coupling.reshape(-1)
    factors = []
    x = initial_state
    edges = edges_of(x)
    for step in range(STEPS):
        x, dfac, *kernel_edges = forward_step(cpl, x, coefficients, edge_halos(*edges, wind_flip))
        factors.append(dfac)
        edges = squeezed(kernel_edges)

    n_lon = lax.axis_size("lon")
    rows = obs_cell.shape[1]
    band = obs_band[0, :, 0]
    valid = jnp.arange(rows, dtype=jnp.int32) < obs_count[0, 0]
    weight = jnp.where(valid, obs_weight[0], 0.0)
    ids = jnp.arange(rows, dtype=jnp.int32)
    same = (band[:, None] == band[None, :]) & (ids[None, :] < ids[:, None])
    rank = jnp.sum(same.astype(jnp.int32), axis=1)
    slot = band * CAP + rank
    payload = jnp.stack([obs_value[0], weight, obs_cell[0].astype(jnp.float32)], axis=1)
    slots = jnp.arange(n_lon * CAP, dtype=jnp.int32)
    hit = slot[None, :] == slots[:, None]
    send = jnp.sum(jnp.where(hit[:, :, None], payload[None, :, :], 0.0), axis=1)
    arrived = lax.all_to_all(send, "lon", 0, 0, tiled=True)
    values = arrived[:, 0]
    weights = arrived[:, 1]
    cells = arrived[:, 2].astype(jnp.int32)
    lanes = x.shape[3]
    row_of = cells // lanes
    lane_of = cells % lanes
    table = x.reshape(-1, lanes)
    lane_hit = lane_of[:, None] == jnp.arange(lanes, dtype=jnp.int32)[None, :]
    picked = jnp.sum(jnp.where(lane_hit, table[row_of], 0.0), axis=1)
    forcing = weights * (picked - values)
    spread = jnp.where(lane_hit, forcing[:, None], 0.0)
    lam = jnp.zeros_like(table).at[row_of].add(spread).reshape(x.shape)

    back_coef = coef_neighbours(coefficients, edge_halos(*edges_of(coefficients), plain_flip))
    lam_y = lam * factors[STEPS - 1]
    edges = edges_of(lam_y)
    for step in range(STEPS - 1, -1, -1):
        last = step == 0
        dprev = factors[step - 1] if not last else factors[0]
        lam_y, *kernel_edges = backward_step(
            cpl, lam_y, coefficients, back_coef, dprev, edge_halos(*edges, wind_flip), last
        )
        edges = squeezed(kernel_edges)
    return (x, lam_y)


def solution(mesh):
    in_specs = (
        P(None, None, "lon", "lat"),
        P(None, None, "lon", "lat"),
        P(),
        P("lat", "lon", None),
        P("lat", "lon"),
        P("lat", "lon"),
        P("lat", "lon"),
        P("lat", "lon"),
    )
    out_specs = (P(None, None, "lon", "lat"), P(None, None, "lon", "lat"))
    return jax.shard_map(
        on_device, mesh=mesh, in_specs=in_specs, out_specs=out_specs, check_vma=False
    )
```

```python
import jax
import jax.numpy as jnp
from jax import lax
from jax.sharding import PartitionSpec as P
from jax.experimental import pallas as pl
from jax.experimental.pallas import tpu as pltpu

STEPS = 2
CAP = 32
UNROLL = 1
LEVEL_BLOCK = 8


def ring_pairs(n_lon, n_lat):
    half = n_lon // 2
    pairs = []
    for i in range(half):
        ring = [(i, j) for j in range(n_lat)] + [(i + half, j) for j in range(n_lat - 1, -1, -1)]
        for k in range(len(ring)):
            a, b = ring[k], ring[(k + 1) % len(ring)]
            pairs.append((a[0] * n_lat + a[1], b[0] * n_lat + b[1]))
    return pairs


def halos(x, flip):
    n_lon = lax.axis_size("lon")
    n_lat = lax.axis_size("lat")
    lon_i = lax.axis_index("lon")
    lat_j = lax.axis_index("lat")
    up = [(i, (i + 1) % n_lon) for i in range(n_lon)]
    down = [(b, a) for a, b in up]
    from_west = lax.ppermute(x[:, :, -1, :], "lon", up)
    from_east = lax.ppermute(x[:, :, 0, :], "lon", down)
    low = lon_i < n_lon // 2
    first_row = x[:, :, :, 0]
    last_row = x[:, :, :, -1]
    cw_pairs = ring_pairs(n_lon, n_lat)
    ccw_pairs = [(b, a) for a, b in cw_pairs]
    cw = lax.ppermute(jnp.where(low, last_row, first_row), ("lon", "lat"), cw_pairs)
    ccw = lax.ppermute(jnp.where(low, first_row, last_row), ("lon", "lat"), ccw_pairs)
    north_row = jnp.where(low, cw, ccw)
    south_row = jnp.where(low, ccw, cw)
    north_row = jnp.where(lat_j == 0, flip * north_row, north_row)
    south_row = jnp.where(lat_j == n_lat - 1, flip * south_row, south_row)
    return north_row, south_row, from_west, from_east


def shifted(x, halo):
    north_row, south_row, from_west, from_east = halo
    north = jnp.concatenate([north_row[..., None], x[..., :-1]], axis=3)
    south = jnp.concatenate([x[..., 1:], south_row[..., None]], axis=3)
    west = jnp.concatenate([from_west[:, :, None, :], x[:, :, :-1, :]], axis=2)
    east = jnp.concatenate([x[:, :, 1:, :], from_east[:, :, None, :]], axis=2)
    return north, south, west, east


def mix(coupling, v, transpose):
    out = []
    for g in range(v.shape[0]):
        acc = None
        for f in range(v.shape[0]):
            c = coupling[:, f, g] if transpose else coupling[:, g, f]
            term = c[:, None, None] * v[f]
            acc = term if acc is None else acc + term
        out.append(acc)
    return jnp.stack(out)


def edge_halos(first_col, last_col, first_row, last_row, flip):
    n_lon = lax.axis_size("lon")
    n_lat = lax.axis_size("lat")
    lon_i = lax.axis_index("lon")
    lat_j = lax.axis_index("lat")
    up = [(i, (i + 1) % n_lon) for i in range(n_lon)]
    down = [(b, a) for a, b in up]
    from_west = lax.ppermute(last_col, "lon", up)
    from_east = lax.ppermute(first_col, "lon", down)
    low = lon_i < n_lon // 2
    cw_pairs = ring_pairs(n_lon, n_lat)
    ccw_pairs = [(b, a) for a, b in cw_pairs]
    cw = lax.ppermute(jnp.where(low, last_row, first_row), ("lon", "lat"), cw_pairs)
    ccw = lax.ppermute(jnp.where(low, first_row, last_row), ("lon", "lat"), ccw_pairs)
    north_row = jnp.where(low, cw, ccw)
    south_row = jnp.where(low, ccw, cw)
    north_row = jnp.where(lat_j == 0, flip * north_row, north_row)
    south_row = jnp.where(lat_j == n_lat - 1, flip * south_row, south_row)
    return (jnp.stack([north_row, south_row], axis=-1), from_west[:, :, None, :], from_east[:, :, None, :])


def edge_masks(shape):
    rows = lax.broadcasted_iota(jnp.int32, shape, 1)
    cols = lax.broadcasted_iota(jnp.int32, shape, 0)
    return rows == 0, rows == shape[1] - 1, cols == 0, cols == shape[0] - 1


def neighbours_2d(v, masks, hn, hs, hw, he):
    c_n, r_n = v.shape
    top, bottom, left, right = masks
    north = jnp.where(top, hn, pltpu.roll(v, 1, 1))
    south = jnp.where(bottom, hs, pltpu.roll(v, r_n - 1, 1))
    west = jnp.where(left, hw, pltpu.roll(v, 1, 0))
    east = jnp.where(right, he, pltpu.roll(v, c_n - 1, 0))
    return north, south, west, east


def write_edges(v, f, l, fc, lc, frl):
    fc[f, l] = v[0:1, :]
    lc[f, l] = v[-1:, :]
    frl[f, l, :, 0:1] = v[:, 0:1]
    frl[f, l, :, 1:2] = v[:, -1:]


def forward_kernel(cpl, x_ref, c_ref, hns, hw, he, xn_ref, d_ref, fc, lc, frl):
    nf = x_ref.shape[0]
    masks = edge_masks(x_ref.shape[2:])

    def body(l, carry):
        lev = pl.program_id(0) * x_ref.shape[1] + l
        xs = [x_ref[f, l] for f in range(nf)]
        cs = [c_ref[d, l] for d in range(4)]
        total = cs[0] + cs[1] + cs[2] + cs[3]
        for g in range(nf):
            v = xs[g]
            north, south, west, east = neighbours_2d(v, masks, hns[g, l, :, 0:1], hns[g, l, :, 1:2], hw[g, l], he[g, l])
            mixed = cpl[lev * nf * nf + g * nf] * xs[0]
            for f in range(1, nf):
                mixed = mixed + cpl[lev * nf * nf + g * nf + f] * xs[f]
            y = v + cs[0] * north + cs[1] * south + cs[2] * west + cs[3] * east - total * v + 0.25 * mixed
            t = jnp.tanh(y)
            xn = y - 0.5 * t
            xn_ref[g, l] = xn
            d_ref[g, l] = 1.0 - 0.5 * (1.0 - t * t)
            write_edges(xn, g, l, fc, lc, frl)
        return carry

    lax.fori_loop(0, x_ref.shape[1], body, 0, unroll=UNROLL)


def backward_kernel(cpl, ly_ref, c_ref, b_ref, dp_ref, hns, hw, he, out_ref, *edge_refs, last):
    nf = ly_ref.shape[0]
    masks = edge_masks(ly_ref.shape[2:])

    def body(l, carry):
        lev = pl.program_id(0) * ly_ref.shape[1] + l
        ls = [ly_ref[f, l] for f in range(nf)]
        cs = [c_ref[d, l] for d in range(4)]
        total = cs[0] + cs[1] + cs[2] + cs[3]
        bs = [b_ref[d, l] for d in range(4)]
        for o in range(nf):
            v = ls[o]
            north, south, west, east = neighbours_2d(v, masks, hns[o, l, :, 0:1], hns[o, l, :, 1:2], hw[o, l], he[o, l])
            back = cpl[lev * nf * nf + o] * ls[0]
            for g in range(1, nf):
                back = back + cpl[lev * nf * nf + g * nf + o] * ls[g]
            lam = v - total * v + 0.25 * back + bs[0] * north + bs[1] * south + bs[2] * west + bs[3] * east
            if last:
                out_ref[o, l] = lam
            else:
                nxt = lam * dp_ref[o, l]
                out_ref[o, l] = nxt
                write_edges(nxt, o, l, *edge_refs)
        return carry

    lax.fori_loop(0, ly_ref.shape[1], body, 0, unroll=UNROLL)


def edge_shapes(x):
    f, l, c, r = x.shape
    return [
        jax.ShapeDtypeStruct((f, l, 1, r), x.dtype),
        jax.ShapeDtypeStruct((f, l, 1, r), x.dtype),
        jax.ShapeDtypeStruct((f, l, c, 2), x.dtype),
    ]


def level_specs(arrays):
    specs = []
    for a in arrays:
        block = (a.shape[0], LEVEL_BLOCK) + tuple(a.shape[2:])
        specs.append(pl.BlockSpec(block, lambda i: (0, i, 0, 0)))
    return specs


def forward_step(cpl, x, coef, halo):
    outs = [jax.ShapeDtypeStruct(x.shape, x.dtype)] * 2 + edge_shapes(x)
    ins = [x, coef, *halo]
    return pl.pallas_call(
        forward_kernel,
        out_shape=outs,
        grid=(x.shape[1] // LEVEL_BLOCK,),
        in_specs=[pl.BlockSpec(memory_space=pltpu.SMEM)] + level_specs(ins),
        out_specs=level_specs(outs),
    )(cpl, *ins)


def backward_step(cpl, ly, coef, back_coef, dprev, halo, last):
    outs = [jax.ShapeDtypeStruct(ly.shape, ly.dtype)] + ([] if last else edge_shapes(ly))
    ins = [ly, coef, back_coef, dprev, *halo]
    return pl.pallas_call(
        lambda *refs: backward_kernel(*refs, last=last),
        out_shape=outs,
        grid=(ly.shape[1] // LEVEL_BLOCK,),
        in_specs=[pl.BlockSpec(memory_space=pltpu.SMEM)] + level_specs(ins),
        out_specs=level_specs(outs),
    )(cpl, *ins)


def edges_of(x):
    return (x[:, :, 0, :], x[:, :, -1, :], x[:, :, :, 0], x[:, :, :, -1])


def squeezed(edges):
    fc, lc, frl = edges
    return (fc[:, :, 0, :], lc[:, :, 0, :], frl[..., 0], frl[..., 1])


def on_device(
    initial_state, coefficients, coupling, obs_band, obs_cell, obs_value, obs_weight, obs_count
):
    wind_flip = jnp.array([-1.0, -1.0, 1.0, 1.0], dtype=jnp.float32).reshape(4, 1, 1)
    plain_flip = jnp.ones((4, 1, 1), jnp.float32)
    cpl = coupling.reshape(-1)
    factors = []
    x = initial_state
    edges = edges_of(x)
    for step in range(STEPS):
        x, dfac, *kernel_edges = forward_step(cpl, x, coefficients, edge_halos(*edges, wind_flip))
        factors.append(dfac)
        edges = squeezed(kernel_edges)

    n_lon = lax.axis_size("lon")
    rows = obs_cell.shape[1]
    band = obs_band[0, :, 0]
    valid = jnp.arange(rows, dtype=jnp.int32) < obs_count[0, 0]
    weight = jnp.where(valid, obs_weight[0], 0.0)
    ids = jnp.arange(rows, dtype=jnp.int32)
    same = (band[:, None] == band[None, :]) & (ids[None, :] < ids[:, None])
    rank = jnp.sum(same.astype(jnp.int32), axis=1)
    slot = band * CAP + rank
    payload = jnp.stack([obs_value[0], weight, obs_cell[0].astype(jnp.float32)], axis=1)
    slots = jnp.arange(n_lon * CAP, dtype=jnp.int32)
    hit = slot[None, :] == slots[:, None]
    send = jnp.sum(jnp.where(hit[:, :, None], payload[None, :, :], 0.0), axis=1)
    arrived = lax.all_to_all(send, "lon", 0, 0, tiled=True)
    values = arrived[:, 0]
    weights = arrived[:, 1]
    cells = arrived[:, 2].astype(jnp.int32)
    lanes = x.shape[3]
    row_of = cells // lanes
    lane_of = cells % lanes
    table = x.reshape(-1, lanes)
    lane_hit = lane_of[:, None] == jnp.arange(lanes, dtype=jnp.int32)[None, :]
    picked = jnp.sum(jnp.where(lane_hit, table[row_of], 0.0), axis=1)
    forcing = weights * (picked - values)
    spread = jnp.where(lane_hit, forcing[:, None], 0.0)
    lam = jnp.zeros_like(table).at[row_of].add(spread).reshape(x.shape)

    near_n, near_s, near_w, near_e = shifted(coefficients, halos(coefficients, plain_flip))
    row_ids = jnp.arange(coefficients.shape[3], dtype=jnp.int32)[None, :]
    polar_top = (lax.axis_index("lat") == 0) & (row_ids == 0)
    polar_bottom = (lax.axis_index("lat") == lax.axis_size("lat") - 1) & (
        row_ids == coefficients.shape[3] - 1
    )
    back_coef = jnp.stack([
        jnp.where(polar_top, near_n[0], near_n[1]),
        jnp.where(polar_bottom, near_s[1], near_s[0]),
        near_w[3],
        near_e[2],
    ])
    lam_y = lam * factors[STEPS - 1]
    edges = edges_of(lam_y)
    for step in range(STEPS - 1, -1, -1):
        last = step == 0
        dprev = factors[step - 1] if not last else factors[0]
        lam_y, *kernel_edges = backward_step(
            cpl, lam_y, coefficients, back_coef, dprev, edge_halos(*edges, wind_flip), last
        )
        if not last:
            edges = squeezed(kernel_edges)
    return (x, lam_y)


def solution(mesh):
    in_specs = (
        P(None, None, "lon", "lat"),
        P(None, None, "lon", "lat"),
        P(),
        P("lat", "lon", None),
        P("lat", "lon"),
        P("lat", "lon"),
        P("lat", "lon"),
        P("lat", "lon"),
    )
    out_specs = (P(None, None, "lon", "lat"), P(None, None, "lon", "lat"))
    return jax.shard_map(
        on_device, mesh=mesh, in_specs=in_specs, out_specs=out_specs, check_vma=False
    )
```
